512 devices in a mesh: tm: 64 (over y, x, core), lat: 8 (over z).
Axes of the slice: x: 4, y: 8, z: 8, core: 2. Of those that a mesh axis runs over, the one named last changes fastest.
Arguments:
- trajectory: float32 [128, 3, 128, 320], P('tm', None, 'lat'), may hold values from -6 to 6
- forcing: float32 [128, 3, 128, 320], P('tm', None, 'lat'), may hold values from -6 to 6
- initial_state: float32 [3, 128, 320], P(None, 'lat'), may hold values from -6 to 6
- depth: float32 [128, 320], P('lat'), may hold values from 0.5 to 2
- warm_start: float32 [192, 3, 2, 128, 320], P('tm', None, None, 'lat'), may hold values from -6 to 6
- slot_unit: int32 [64, 3], replicated, may hold values from 0 to 63, as said below
- unit_count: int32 [64], replicated, may hold values from 0 to 3, as said below
Outputs:
- updated: float32 [3, 128, 320, 128], P(None, 'lat', 'tm')
- spectrum: float32 [192, 3, 2, 128, 320], P('tm', None, None, 'lat')
The draws below stay inside these ranges and needn't reach their ends.
Inputs may be any that keep to these rules, and one draw needn't show every extreme that they name: Owner d holds the pairs slot_unit[d, 0 .. unit_count[d] - 1]; every pair 0 .. 63 is held exactly once over all owners; slots at or past unit_count[d] hold 0. `unit_count`: 8 owners hold 3 pairs, 8 hold 2, 24 hold 1 and the others none; which owners is drawn.
All inputs are finite; a program needn't handle non-finite values.
Results may differ from the reference program's by a relative error of at most 0.0003.
Values sent between devices are 32-bit elements; how exact they have to be, the bound alone decides.
No kernel may reach another device: no remote copies, remote signals or barrier semaphores. Data moves between devices by JAX's collectives and lax.ppermute only.
A program may use at most 64 MiB of HBM per device.

```python
import math
import jax
import jax.numpy as jnp
from jax import lax

NX = 320
CAP = 3
SWEEPS = 6
NY = 128
STEPS = 128
UNITS = 64
OWNERS = 64


def owner_layout(key):
    base_key = jax.random.fold_in(key, 4242)
    count_key, unit_key = jax.random.split(base_key)
    eighth = OWNERS // 8
    pattern = jnp.concatenate([jnp.full((eighth,), 3, jnp.int32), jnp.full((eighth,), 2, jnp.int32), jnp.full((3 * eighth,), 1, jnp.int32), jnp.zeros((OWNERS - 5 * eighth,), jnp.int32)])
    counts = jax.random.permutation(count_key, pattern)
    ordering = jax.random.permutation(unit_key, UNITS).astype(jnp.int32)
    starts = jnp.cumsum(counts) - counts
    slot_ids = jnp.arange(CAP, dtype=jnp.int32)
    position = starts[:, None] + slot_ids[None, :]
    filled = slot_ids[None, :] < counts[:, None]
    table = jnp.where(filled, ordering[jnp.minimum(position, UNITS - 1)], 0)
    return (table.astype(jnp.int32), counts.astype(jnp.int32))


def draw_slot_unit(key, part):
    return owner_layout(key)[0]


def draw_unit_count(key, part):
    return owner_layout(key)[1]


def steps_of(stream_key, dims, pieces, low, high):
    level, own = 1.0, jax.random.fold_in(stream_key, 6)
    for dim, shards_of in pieces:
        heights = jnp.exp(jax.random.uniform(jax.random.fold_in(own, dim), (shards_of,), jnp.float32, low / len(pieces), high / len(pieces)))
        level = level * jnp.repeat(heights, dims[dim] // shards_of).reshape([-1 if axis == dim else 1 for axis in range(len(dims))])
    return level


def centred(own_key, dims, spread, bound, pieces=(), kind=jnp.bfloat16):
    gain = steps_of(own_key, dims, pieces, -0.22, 0.18) if pieces else 1.0
    entries = jax.random.normal(own_key, dims, jnp.float32) * spread * gain
    return jnp.minimum(jnp.maximum(entries, -bound), bound).astype(kind)


def setup_inputs(seed: int = 0) -> dict:
    streams_of = jax.random.split(jax.random.key(seed), 8)
    trajectory = centred(streams_of[0], (STEPS, 3, NY, NX), 1.0, 6.0, ((0, 64), (2, 8)), jnp.float32)
    forcing = centred(streams_of[1], (STEPS, 3, NY, NX), 1.0, 6.0, ((0, 64), (2, 8)), jnp.float32)
    initial_state = centred(streams_of[2], (3, NY, NX), 1.0, 6.0, ((1, 8),), jnp.float32)
    depth = jnp.clip(jnp.exp(math.log(2.0) - 1.3862944 * jax.random.uniform(streams_of[3], (NY, NX), jnp.float32) ** steps_of(streams_of[3], (NY, NX), ((0, 8),), -0.2, 0.2)), 0.5, 2.0)
    warm_start = centred(streams_of[4], (OWNERS * CAP, 3, 2, NY, NX), 1.0, 6.0, ((0, 64), (3, 8)), jnp.float32)
    slot_unit = draw_slot_unit(jax.random.fold_in(streams_of[7], 71), 0)
    unit_count = draw_unit_count(jax.random.fold_in(streams_of[7], 71), 0)
    return {"trajectory": trajectory, "forcing": forcing, "initial_state": initial_state, "depth": depth, "warm_start": warm_start, "slot_unit": slot_unit, "unit_count": unit_count}


HALF_COUPLING = 0.125
CORIOLIS = 0.2
FRICTION = 1.0
ALPHA = 0.1
SPREAD = 0.2

def zero_rim(values):
    widths = [(0, 0)] * (values.ndim - 2) + [(1, 1), (1, 1)]
    return jnp.pad(values, widths)

def flux_operator(state, depth, pad_rule):
    height = state[..., 0:1, :, :, :]
    east = state[..., 1:2, :, :, :]
    north = state[..., 2:3, :, :, :]
    flux = jnp.concatenate([height, depth * east, depth * north], axis=-4)
    padded = pad_rule(flux)
    grad_x = padded[..., 0:1, :, 1:-1, 2:] - padded[..., 0:1, :, 1:-1, :-2]
    grad_y = padded[..., 0:1, :, 2:, 1:-1] - padded[..., 0:1, :, :-2, 1:-1]
    diverge = padded[..., 1:2, :, 1:-1, 2:] - padded[..., 1:2, :, 1:-1, :-2] + (padded[..., 2:3, :, 2:, 1:-1] - padded[..., 2:3, :, :-2, 1:-1])
    new_height = HALF_COUPLING * diverge
    new_east = HALF_COUPLING * grad_x - CORIOLIS * north
    new_north = HALF_COUPLING * grad_y + CORIOLIS * east
    return jnp.concatenate([new_height, new_east, new_north], axis=-4)

def time_tables(step_count, pair_count):
    index_t = jnp.arange(step_count, dtype=jnp.int32)
    index_k = jnp.arange(pair_count, dtype=jnp.int32)
    phases = index_t[:, None] * index_k[None, :] % step_count
    angles = phases.astype(jnp.float32) * (2.0 * math.pi / step_count)
    cosine = jnp.cos(angles)
    sine = jnp.sin(angles)
    parity = (1 - 2 * (index_t % 2)).astype(jnp.float32)
    first = index_k == 0
    times = index_t.astype(jnp.float32) / step_count
    damping = jnp.exp(times * math.log(ALPHA)) / math.sqrt(step_count)
    growth = jnp.exp(-times * math.log(ALPHA)) / math.sqrt(step_count)
    forward_imag = jnp.where(first[None, :], parity[:, None], -sine)
    forward_table = jnp.concatenate([cosine, forward_imag], axis=1) * damping[:, None]
    weights = jnp.where(first, 1.0, 2.0).astype(jnp.float32)
    inverse_real = (cosine * weights[None, :]).T
    inverse_imag = jnp.where(first[None, :], parity[:, None], -2.0 * sine).T
    inverse_table = jnp.concatenate([inverse_real, inverse_imag], axis=0) * growth[None, :]
    return (forward_table, inverse_table)

def unit_inverse(pair_ids, step_count):
    angles = pair_ids.astype(jnp.float32) * (2.0 * math.pi / step_count)
    ratio = math.exp(math.log(ALPHA) / step_count)
    real_shift = 1.0 + FRICTION - ratio * jnp.cos(angles)
    imag_shift = ratio * jnp.sin(angles)
    denominator = real_shift * real_shift + imag_shift * imag_shift
    real_inv = real_shift / denominator
    imag_inv = -imag_shift / denominator
    is_first = pair_ids == 0
    upper_left = jnp.where(is_first, 1.0 / (1.0 + FRICTION - ratio), real_inv)
    upper_right = jnp.where(is_first, 0.0, -imag_inv)
    lower_left = jnp.where(is_first, 0.0, imag_inv)
    lower_right = jnp.where(is_first, 1.0 / (1.0 + FRICTION + ratio), real_inv)
    return (upper_left, upper_right, lower_left, lower_right)

def apply_inverse(coeffs, values):
    shaped = [c[:, None, None, None] for c in coeffs]
    real_part = values[:, :, 0]
    imag_part = values[:, :, 1]
    new_real = shaped[0] * real_part + shaped[1] * imag_part
    new_imag = shaped[2] * real_part + shaped[3] * imag_part
    return jnp.stack([new_real, new_imag], axis=2)

def chebyshev(source, start, depth, coeffs, pad_rule):
    iterate = start
    for sweep in range(SWEEPS):
        weight = 1.0 / (1.0 + SPREAD * math.cos(math.pi * (2 * sweep + 1) / (2 * SWEEPS)))
        update = apply_inverse(coeffs, source - flux_operator(iterate, depth, pad_rule)) - iterate
        iterate = iterate + weight * update
    return iterate

def placement(slot_unit, unit_count, pair_count):
    owner_total, slot_total = slot_unit.shape
    flat_units = slot_unit.reshape(-1)
    filled = (jnp.arange(slot_total, dtype=jnp.int32)[None, :] < unit_count[:, None]).reshape(-1)
    matches = (flat_units[None, :] == jnp.arange(pair_count, dtype=jnp.int32)[:, None]) & filled[None, :]
    slot_ids = jnp.arange(owner_total * slot_total, dtype=jnp.int32)
    slot_of = lax.optimization_barrier(jnp.sum(jnp.where(matches, slot_ids[None, :], 0), axis=1)).astype(jnp.int32)
    return (slot_of, filled, flat_units)

def reference(trajectory, forcing, initial_state, depth, warm_start, slot_unit, unit_count):
    previous = jnp.concatenate([initial_state[None], trajectory[:-1]], axis=0)
    flux_term = flux_operator(trajectory[:, :, None], depth, zero_rim)[:, :, 0]
    resid = forcing - ((1.0 + FRICTION) * trajectory - previous + flux_term)
    forward_table, inverse_table = time_tables(STEPS, UNITS)
    spec = jnp.einsum('tfyx,tk->kfyx', resid, forward_table, precision=lax.Precision.HIGHEST)
    spec = jnp.transpose(spec.reshape(2, UNITS, 3, NY, NX), (1, 2, 0, 3, 4))
    slot_of, filled, flat_units = placement(slot_unit, unit_count, UNITS)
    start = jnp.take(warm_start, slot_of, axis=0)
    coeffs = unit_inverse(jnp.arange(UNITS, dtype=jnp.int32), STEPS)
    solved = chebyshev(spec, start, depth, coeffs, zero_rim)
    spectrum = jnp.where(filled[:, None, None, None, None], jnp.take(solved, flat_units, axis=0), 0.0)
    corr = jnp.einsum('ufryx,rut->fyxt', solved, inverse_table.reshape(2, UNITS, STEPS), precision=lax.Precision.HIGHEST)
    updated = jnp.transpose(trajectory, (1, 2, 3, 0)) + corr
    return (updated, spectrum)
```

```python
import math

import jax
import jax.numpy as jnp
from jax import lax
from jax.sharding import PartitionSpec as P

SWEEPS = 6


HALF_COUPLING = 0.125
CORIOLIS = 0.2
FRICTION = 1.0
ALPHA = 0.1
SPREAD = 0.2


def with_halo(cells, sides, width):
    for axis, dim in sides:
        count = lax.axis_size(axis)
        ends = count - 1
        head = lax.slice_in_dim(cells, 0, width, axis=dim)
        tail = lax.slice_in_dim(cells, cells.shape[dim] - width, cells.shape[dim], axis=dim)
        cells = jnp.concatenate(
            [
                lax.ppermute(tail, axis, [(i, (i + 1) % count) for i in range(ends)]),
                cells,
                lax.ppermute(head, axis, [((i + 1) % count, i) for i in range(ends)]),
            ],
            axis=dim,
        )
    return cells


def shifted(value, axis, by):
    size = lax.axis_size(axis)
    pairs = [(i, i + by) for i in range(size) if 0 <= i + by < size]
    return lax.ppermute(value, axis, pairs)


def flux_operator(state, depth, pad_rule, row_mask=None):
    height = state[..., 0:1, :, :, :]
    east = state[..., 1:2, :, :, :]
    north = state[..., 2:3, :, :, :]
    if row_mask is not None:
        height = height * row_mask
    flux = jnp.concatenate([height, depth * east, depth * north], axis=-4)
    padded = pad_rule(flux)
    grad_x = padded[..., 0:1, :, 1:-1, 2:] - padded[..., 0:1, :, 1:-1, :-2]
    grad_y = padded[..., 0:1, :, 2:, 1:-1] - padded[..., 0:1, :, :-2, 1:-1]
    diverge = (
        padded[..., 1:2, :, 1:-1, 2:]
        - padded[..., 1:2, :, 1:-1, :-2]
        + (padded[..., 2:3, :, 2:, 1:-1] - padded[..., 2:3, :, :-2, 1:-1])
    )
    new_height = HALF_COUPLING * diverge
    new_east = HALF_COUPLING * grad_x - CORIOLIS * north
    new_north = HALF_COUPLING * grad_y + CORIOLIS * east
    return jnp.concatenate([new_height, new_east, new_north], axis=-4)


def row_rims(flux):
    rows_done = with_halo(flux, (("lat", 3),), 1)
    return jnp.pad(rows_done, ((0, 0), (0, 0), (0, 0), (0, 0), (1, 1)))


def zero_rim(values):
    widths = [(0, 0)] * (values.ndim - 2) + [(1, 1), (1, 1)]
    return jnp.pad(values, widths)


def to_owners(slots):
    return lax.all_to_all(slots, "tm", split_axis=0, concat_axis=4, tiled=True)


def from_owners(slots):
    return lax.all_to_all(slots, "tm", split_axis=4, concat_axis=0, tiled=True)


def slot_tables(units, filled, step_count):
    index_t = jnp.arange(step_count, dtype=jnp.int32)
    phases = index_t[:, None] * units[None, :] % step_count
    angles = phases.astype(jnp.float32) * (2.0 * math.pi / step_count)
    cosine = jnp.cos(angles)
    sine = jnp.sin(angles)
    parity = (1 - 2 * (index_t % 2)).astype(jnp.float32)
    first = units == 0
    times = index_t.astype(jnp.float32) / step_count
    damping = jnp.exp(times * math.log(ALPHA)) / math.sqrt(step_count)
    growth = jnp.exp(-times * math.log(ALPHA)) / math.sqrt(step_count)
    forward_imag = jnp.where(first[None, :], parity[:, None], -sine)
    forward_table = jnp.stack([cosine, forward_imag], axis=2) * damping[:, None, None]
    weights = jnp.where(first, 1.0, 2.0).astype(jnp.float32)
    inverse_real = cosine * weights[None, :]
    inverse_imag = jnp.where(first[None, :], parity[:, None], -2.0 * sine)
    keep = filled.astype(jnp.float32)[None, :, None]
    inverse_table = jnp.stack([inverse_real, inverse_imag], axis=2) * growth[:, None, None] * keep
    return (forward_table, inverse_table)


def unit_inverse(pair_ids, step_count):
    angles = pair_ids.astype(jnp.float32) * (2.0 * math.pi / step_count)
    ratio = math.exp(math.log(ALPHA) / step_count)
    real_shift = 1.0 + FRICTION - ratio * jnp.cos(angles)
    imag_shift = ratio * jnp.sin(angles)
    denominator = real_shift * real_shift + imag_shift * imag_shift
    real_inv = real_shift / denominator
    imag_inv = -imag_shift / denominator
    is_first = pair_ids == 0
    upper_left = jnp.where(is_first, 1.0 / (1.0 + FRICTION - ratio), real_inv)
    upper_right = jnp.where(is_first, 0.0, -imag_inv)
    lower_left = jnp.where(is_first, 0.0, imag_inv)
    lower_right = jnp.where(is_first, 1.0 / (1.0 + FRICTION + ratio), real_inv)
    return (upper_left, upper_right, lower_left, lower_right)


def apply_inverse(coeffs, values):
    shaped = [c[:, None, None, None] for c in coeffs]
    real_part = values[:, :, 0]
    imag_part = values[:, :, 1]
    new_real = shaped[0] * real_part + shaped[1] * imag_part
    new_imag = shaped[2] * real_part + shaped[3] * imag_part
    return jnp.stack([new_real, new_imag], axis=2)


def chebyshev(source, start, depth, coeffs, row_mask):
    iterate = start
    for sweep in range(SWEEPS):
        weight = 1.0 / (1.0 + SPREAD * math.cos(math.pi * (2 * sweep + 1) / (2 * SWEEPS)))
        flux = flux_operator(iterate, depth, zero_rim, row_mask)
        update = apply_inverse(coeffs, source - flux) - iterate
        iterate = iterate + weight * update
    return iterate


def body(trajectory, forcing, initial_state, depth, warm_start, slot_unit, unit_count):
    groups = lax.axis_size("tm")
    position = lax.axis_index("tm")
    local_steps = trajectory.shape[0]
    step_count = local_steps * groups
    rows = depth.shape[0]
    lat_count = lax.axis_size("lat")
    lat_pos = lax.axis_index("lat")
    width = SWEEPS

    last_step = shifted(trajectory[local_steps - 1], "tm", 1)
    first_previous = jnp.where(position == 0, initial_state, last_step)
    previous = jnp.concatenate([first_previous[None], trajectory[: local_steps - 1]], axis=0)
    flux_term = flux_operator(trajectory[:, :, None], depth, row_rims)[:, :, 0]
    resid = forcing - ((1.0 + FRICTION) * trajectory - previous + flux_term)
    moved_state, moved_resid = (
        lax.all_to_all(trajectory, "tm", split_axis=3, concat_axis=0, tiled=True),
        lax.all_to_all(resid, "tm", split_axis=3, concat_axis=0, tiled=True),
    )
    state_cols = jnp.transpose(moved_state, (1, 2, 3, 0))
    fields, col_count = moved_resid.shape[1], moved_resid.shape[3]

    flat_units = slot_unit.reshape(-1)
    slot_total = slot_unit.shape[1]
    filled = (jnp.arange(slot_total, dtype=jnp.int32)[None, :] < unit_count[:, None]).reshape(-1)
    forward_table, inverse_table = slot_tables(flat_units, filled, step_count)

    outgoing = jnp.einsum(
        "tsp,tfyx->sfpyx", forward_table, moved_resid, precision=lax.Precision.HIGHEST
    )
    source = to_owners(outgoing)

    own_units = lax.dynamic_index_in_dim(slot_unit, position, 0, keepdims=False)
    own_filled = lax.dynamic_index_in_dim(filled.reshape(groups, -1), position, 0, keepdims=False)
    coeffs = unit_inverse(own_units, step_count)

    wide_source = with_halo(source, (("lat", 3),), width)
    wide_start = with_halo(warm_start, (("lat", 3),), width)
    wide_depth = with_halo(depth, (("lat", 0),), width)
    global_row = lat_pos * rows - width + jnp.arange(rows + 2 * width, dtype=jnp.int32)
    row_mask = ((global_row >= 0) & (global_row < rows * lat_count)).astype(jnp.float32)
    solved = chebyshev(wide_source, wide_start, wide_depth, coeffs, row_mask[:, None])
    solved = solved[:, :, :, width : width + rows]
    spectrum = jnp.where(own_filled[:, None, None, None, None], solved, 0.0)

    solved_cols = from_owners(solved)
    corr = jnp.einsum(
        "sfpyx,tsp->fyxt", solved_cols, inverse_table, precision=lax.Precision.HIGHEST
    )
    updated = state_cols + corr
    return (updated, spectrum)


def solution(mesh):
    return jax.shard_map(
        body,
        mesh=mesh,
        in_specs=(
            P("tm", None, "lat", None),
            P("tm", None, "lat", None),
            P(None, "lat", None),
            P("lat", None),
            P("tm", None, None, "lat", None),
            P(),
            P(),
        ),
        out_specs=(P(None, "lat", "tm", None), P("tm", None, None, "lat", None)),
        check_vma=False,
    )
```

```python
import math

import jax
import jax.numpy as jnp
from jax import lax
from jax.sharding import PartitionSpec as P

SWEEPS = 6


HALF_COUPLING = 0.125
CORIOLIS = 0.2
FRICTION = 1.0
ALPHA = 0.1
SPREAD = 0.2


def with_halo(cells, sides, width):
    for axis, dim in sides:
        count = lax.axis_size(axis)
        ends = count - 1
        head = lax.slice_in_dim(cells, 0, width, axis=dim)
        tail = lax.slice_in_dim(cells, cells.shape[dim] - width, cells.shape[dim], axis=dim)
        cells = jnp.concatenate(
            [
                lax.ppermute(tail, axis, [(i, (i + 1) % count) for i in range(ends)]),
                cells,
                lax.ppermute(head, axis, [((i + 1) % count, i) for i in range(ends)]),
            ],
            axis=dim,
        )
    return cells


def shifted(value, axis, by):
    size = lax.axis_size(axis)
    pairs = [(i, i + by) for i in range(size) if 0 <= i + by < size]
    return lax.ppermute(value, axis, pairs)


def flux_operator(state, depth, pad_rule, row_mask=None):
    height = state[..., 0:1, :, :, :]
    east = state[..., 1:2, :, :, :]
    north = state[..., 2:3, :, :, :]
    if row_mask is not None:
        height = height * row_mask
    flux = jnp.concatenate([height, depth * east, depth * north], axis=-4)
    padded = pad_rule(flux)
    grad_x = padded[..., 0:1, :, 1:-1, 2:] - padded[..., 0:1, :, 1:-1, :-2]
    grad_y = padded[..., 0:1, :, 2:, 1:-1] - padded[..., 0:1, :, :-2, 1:-1]
    diverge = (
        padded[..., 1:2, :, 1:-1, 2:]
        - padded[..., 1:2, :, 1:-1, :-2]
        + (padded[..., 2:3, :, 2:, 1:-1] - padded[..., 2:3, :, :-2, 1:-1])
    )
    new_height = HALF_COUPLING * diverge
    new_east = HALF_COUPLING * grad_x - CORIOLIS * north
    new_north = HALF_COUPLING * grad_y + CORIOLIS * east
    return jnp.concatenate([new_height, new_east, new_north], axis=-4)


def row_rims(flux):
    rows_done = with_halo(flux, (("lat", 3),), 1)
    return jnp.pad(rows_done, ((0, 0), (0, 0), (0, 0), (0, 0), (1, 1)))


def zero_rim(values):
    widths = [(0, 0)] * (values.ndim - 2) + [(1, 1), (1, 1)]
    return jnp.pad(values, widths)


def to_owners(slots):
    return lax.all_to_all(slots, "tm", split_axis=0, concat_axis=4, tiled=True)


def from_owners(slots):
    return lax.all_to_all(slots, "tm", split_axis=4, concat_axis=0, tiled=True)


def slot_tables(units, filled, step_count):
    index_t = jnp.arange(step_count, dtype=jnp.int32)
    phases = index_t[:, None] * units[None, :] % step_count
    angles = phases.astype(jnp.float32) * (2.0 * math.pi / step_count)
    cosine = jnp.cos(angles)
    sine = jnp.sin(angles)
    parity = (1 - 2 * (index_t % 2)).astype(jnp.float32)
    first = units == 0
    times = index_t.astype(jnp.float32) / step_count
    damping = jnp.exp(times * math.log(ALPHA)) / math.sqrt(step_count)
    growth = jnp.exp(-times * math.log(ALPHA)) / math.sqrt(step_count)
    forward_imag = jnp.where(first[None, :], parity[:, None], -sine)
    forward_table = jnp.stack([cosine, forward_imag], axis=2) * damping[:, None, None]
    weights = jnp.where(first, 1.0, 2.0).astype(jnp.float32)
    inverse_real = cosine * weights[None, :]
    inverse_imag = jnp.where(first[None, :], parity[:, None], -2.0 * sine)
    keep = filled.astype(jnp.float32)[None, :, None]
    inverse_table = jnp.stack([inverse_real, inverse_imag], axis=2) * growth[:, None, None] * keep
    return (forward_table, inverse_table)


def unit_inverse(pair_ids, step_count):
    angles = pair_ids.astype(jnp.float32) * (2.0 * math.pi / step_count)
    ratio = math.exp(math.log(ALPHA) / step_count)
    real_shift = 1.0 + FRICTION - ratio * jnp.cos(angles)
    imag_shift = ratio * jnp.sin(angles)
    denominator = real_shift * real_shift + imag_shift * imag_shift
    real_inv = real_shift / denominator
    imag_inv = -imag_shift / denominator
    is_first = pair_ids == 0
    upper_left = jnp.where(is_first, 1.0 / (1.0 + FRICTION - ratio), real_inv)
    upper_right = jnp.where(is_first, 0.0, -imag_inv)
    lower_left = jnp.where(is_first, 0.0, imag_inv)
    lower_right = jnp.where(is_first, 1.0 / (1.0 + FRICTION + ratio), real_inv)
    return (upper_left, upper_right, lower_left, lower_right)


def apply_inverse(coeffs, values):
    shaped = [c[:, None, None, None] for c in coeffs]
    real_part = values[:, :, 0]
    imag_part = values[:, :, 1]
    new_real = shaped[0] * real_part + shaped[1] * imag_part
    new_imag = shaped[2] * real_part + shaped[3] * imag_part
    return jnp.stack([new_real, new_imag], axis=2)


def chebyshev(source, start, depth, coeffs, row_mask):
    iterate = start
    for sweep in range(SWEEPS):
        weight = 1.0 / (1.0 + SPREAD * math.cos(math.pi * (2 * sweep + 1) / (2 * SWEEPS)))
        flux = flux_operator(iterate, depth, zero_rim, row_mask)
        update = apply_inverse(coeffs, source - flux) - iterate
        iterate = iterate + weight * update
    return iterate


def body(trajectory, forcing, initial_state, depth, warm_start, slot_unit, unit_count):
    groups = lax.axis_size("tm")
    position = lax.axis_index("tm")
    local_steps = trajectory.shape[0]
    step_count = local_steps * groups
    rows = depth.shape[0]
    lat_count = lax.axis_size("lat")
    lat_pos = lax.axis_index("lat")
    width = 8 * ((SWEEPS + 7) // 8)

    last_step = shifted(trajectory[local_steps - 1], "tm", 1)
    first_previous = jnp.where(position == 0, initial_state, last_step)
    previous = jnp.concatenate([first_previous[None], trajectory[: local_steps - 1]], axis=0)
    flux_term = flux_operator(trajectory[:, :, None], depth, row_rims)[:, :, 0]
    resid = forcing - ((1.0 + FRICTION) * trajectory - previous + flux_term)
    moved_state, moved_resid = (
        lax.all_to_all(trajectory, "tm", split_axis=3, concat_axis=0, tiled=True),
        lax.all_to_all(resid, "tm", split_axis=3, concat_axis=0, tiled=True),
    )
    state_cols = jnp.transpose(moved_state, (1, 2, 3, 0))
    fields, col_count = moved_resid.shape[1], moved_resid.shape[3]

    flat_units = slot_unit.reshape(-1)
    slot_total = slot_unit.shape[1]
    filled = (jnp.arange(slot_total, dtype=jnp.int32)[None, :] < unit_count[:, None]).reshape(-1)
    forward_table, inverse_table = slot_tables(flat_units, filled, step_count)

    outgoing = jnp.einsum(
        "tsp,tfyx->sfpyx", forward_table, moved_resid, precision=lax.Precision.HIGHEST
    )
    source = to_owners(outgoing)

    own_units = lax.dynamic_index_in_dim(slot_unit, position, 0, keepdims=False)
    own_filled = lax.dynamic_index_in_dim(filled.reshape(groups, -1), position, 0, keepdims=False)
    coeffs = unit_inverse(own_units, step_count)

    wide_source = with_halo(source, (("lat", 3),), width)
    wide_start = with_halo(warm_start, (("lat", 3),), width)
    wide_depth = with_halo(depth, (("lat", 0),), width)
    global_row = lat_pos * rows - width + jnp.arange(rows + 2 * width, dtype=jnp.int32)
    row_mask = ((global_row >= 0) & (global_row < rows * lat_count)).astype(jnp.float32)
    solved = chebyshev(wide_source, wide_start, wide_depth, coeffs, row_mask[:, None])
    solved = solved[:, :, :, width : width + rows]
    spectrum = jnp.where(own_filled[:, None, None, None, None], solved, 0.0)

    solved_cols = from_owners(solved)
    corr = jnp.einsum(
        "sfpyx,tsp->fyxt", solved_cols, inverse_table, precision=lax.Precision.HIGHEST
    )
    updated = state_cols + corr
    return (updated, spectrum)


def solution(mesh):
    return jax.shard_map(
        body,
        mesh=mesh,
        in_specs=(
            P("tm", None, "lat", None),
            P("tm", None, "lat", None),
            P(None, "lat", None),
            P("lat", None),
            P("tm", None, None, "lat", None),
            P(),
            P(),
        ),
        out_specs=(P(None, "lat", "tm", None), P("tm", None, None, "lat", None)),
        check_vma=False,
    )
```

```python
import math

import jax
import jax.numpy as jnp
from jax import lax
from jax.sharding import PartitionSpec as P

SWEEPS = 6


HALF_COUPLING = 0.125
CORIOLIS = 0.2
FRICTION = 1.0
ALPHA = 0.1
SPREAD = 0.2


def with_halo(cells, sides, width):
    for axis, dim in sides:
        count = lax.axis_size(axis)
        ends = count - 1
        head = lax.slice_in_dim(cells, 0, width, axis=dim)
        tail = lax.slice_in_dim(cells, cells.shape[dim] - width, cells.shape[dim], axis=dim)
        cells = jnp.concatenate(
            [
                lax.ppermute(tail, axis, [(i, (i + 1) % count) for i in range(ends)]),
                cells,
                lax.ppermute(head, axis, [((i + 1) % count, i) for i in range(ends)]),
            ],
            axis=dim,
        )
    return cells


def shifted(value, axis, by):
    size = lax.axis_size(axis)
    pairs = [(i, i + by) for i in range(size) if 0 <= i + by < size]
    return lax.ppermute(value, axis, pairs)


def flux_operator(state, depth, pad_rule, row_mask=None):
    height = state[..., 0:1, :, :, :]
    east = state[..., 1:2, :, :, :]
    north = state[..., 2:3, :, :, :]
    if row_mask is not None:
        height = height * row_mask
    flux = jnp.concatenate([height, depth * east, depth * north], axis=-4)
    padded = pad_rule(flux)
    grad_x = padded[..., 0:1, :, 1:-1, 2:] - padded[..., 0:1, :, 1:-1, :-2]
    grad_y = padded[..., 0:1, :, 2:, 1:-1] - padded[..., 0:1, :, :-2, 1:-1]
    diverge = (
        padded[..., 1:2, :, 1:-1, 2:]
        - padded[..., 1:2, :, 1:-1, :-2]
        + (padded[..., 2:3, :, 2:, 1:-1] - padded[..., 2:3, :, :-2, 1:-1])
    )
    new_height = HALF_COUPLING * diverge
    new_east = HALF_COUPLING * grad_x - CORIOLIS * north
    new_north = HALF_COUPLING * grad_y + CORIOLIS * east
    return jnp.concatenate([new_height, new_east, new_north], axis=-4)


def row_rims(flux):
    rows_done = with_halo(flux, (("lat", 3),), 1)
    return jnp.pad(rows_done, ((0, 0), (0, 0), (0, 0), (0, 0), (1, 1)))


def zero_rim(values):
    widths = [(0, 0)] * (values.ndim - 2) + [(1, 1), (1, 1)]
    return jnp.pad(values, widths)


def to_owners(slots):
    return lax.all_to_all(slots, "tm", split_axis=0, concat_axis=4, tiled=True)


def from_owners(slots):
    return lax.all_to_all(slots, "tm", split_axis=4, concat_axis=0, tiled=True)


def slot_tables(units, filled, step_count):
    index_t = jnp.arange(step_count, dtype=jnp.int32)
    phases = index_t[:, None] * units[None, :] % step_count
    angles = phases.astype(jnp.float32) * (2.0 * math.pi / step_count)
    cosine = jnp.cos(angles)
    sine = jnp.sin(angles)
    parity = (1 - 2 * (index_t % 2)).astype(jnp.float32)
    first = units == 0
    times = index_t.astype(jnp.float32) / step_count
    damping = jnp.exp(times * math.log(ALPHA)) / math.sqrt(step_count)
    growth = jnp.exp(-times * math.log(ALPHA)) / math.sqrt(step_count)
    forward_imag = jnp.where(first[None, :], parity[:, None], -sine)
    forward_table = jnp.stack([cosine, forward_imag], axis=2) * damping[:, None, None]
    weights = jnp.where(first, 1.0, 2.0).astype(jnp.float32)
    inverse_real = cosine * weights[None, :]
    inverse_imag = jnp.where(first[None, :], parity[:, None], -2.0 * sine)
    keep = filled.astype(jnp.float32)[None, :, None]
    inverse_table = jnp.stack([inverse_real, inverse_imag], axis=2) * growth[:, None, None] * keep
    return (forward_table, inverse_table)


def unit_inverse(pair_ids, step_count):
    angles = pair_ids.astype(jnp.float32) * (2.0 * math.pi / step_count)
    ratio = math.exp(math.log(ALPHA) / step_count)
    real_shift = 1.0 + FRICTION - ratio * jnp.cos(angles)
    imag_shift = ratio * jnp.sin(angles)
    denominator = real_shift * real_shift + imag_shift * imag_shift
    real_inv = real_shift / denominator
    imag_inv = -imag_shift / denominator
    is_first = pair_ids == 0
    upper_left = jnp.where(is_first, 1.0 / (1.0 + FRICTION - ratio), real_inv)
    upper_right = jnp.where(is_first, 0.0, -imag_inv)
    lower_left = jnp.where(is_first, 0.0, imag_inv)
    lower_right = jnp.where(is_first, 1.0 / (1.0 + FRICTION + ratio), real_inv)
    return (upper_left, upper_right, lower_left, lower_right)


def apply_inverse(coeffs, values):
    shaped = [c[:, None, None, None] for c in coeffs]
    real_part = values[:, :, 0]
    imag_part = values[:, :, 1]
    new_real = shaped[0] * real_part + shaped[1] * imag_part
    new_imag = shaped[2] * real_part + shaped[3] * imag_part
    return jnp.stack([new_real, new_imag], axis=2)


def chebyshev(source, start, depth, coeffs, row_mask):
    iterate = start
    for sweep in range(SWEEPS):
        weight = 1.0 / (1.0 + SPREAD * math.cos(math.pi * (2 * sweep + 1) / (2 * SWEEPS)))
        flux = flux_operator(iterate, depth, zero_rim, row_mask)
        update = apply_inverse(coeffs, source - flux) - iterate
        iterate = iterate + weight * update
    return iterate


def body(trajectory, forcing, initial_state, depth, warm_start, slot_unit, unit_count):
    groups = lax.axis_size("tm")
    position = lax.axis_index("tm")
    local_steps = trajectory.shape[0]
    step_count = local_steps * groups
    rows = depth.shape[0]
    lat_count = lax.axis_size("lat")
    lat_pos = lax.axis_index("lat")
    width = 8 * ((SWEEPS + 7) // 8)

    last_step = shifted(trajectory[local_steps - 1], "tm", 1)
    first_previous = jnp.where(position == 0, initial_state, last_step)
    previous = jnp.concatenate([first_previous[None], trajectory[: local_steps - 1]], axis=0)
    flux_term = flux_operator(trajectory[:, :, None], depth, row_rims)[:, :, 0]
    resid = forcing - ((1.0 + FRICTION) * trajectory - previous + flux_term)
    moved = lax.all_to_all(
        jnp.stack([trajectory, resid], axis=1), "tm", split_axis=4, concat_axis=0, tiled=True
    )
    moved_state, moved_resid = moved[:, 0], moved[:, 1]
    state_cols = jnp.transpose(moved_state, (1, 2, 3, 0))
    fields, col_count = moved_resid.shape[1], moved_resid.shape[3]

    flat_units = slot_unit.reshape(-1)
    slot_total = slot_unit.shape[1]
    filled = (jnp.arange(slot_total, dtype=jnp.int32)[None, :] < unit_count[:, None]).reshape(-1)
    forward_table, inverse_table = slot_tables(flat_units, filled, step_count)

    outgoing = jnp.einsum(
        "tsp,tfyx->sfpyx", forward_table, moved_resid, precision=lax.Precision.HIGHEST
    )
    source = to_owners(outgoing)

    own_units = lax.dynamic_index_in_dim(slot_unit, position, 0, keepdims=False)
    own_filled = lax.dynamic_index_in_dim(filled.reshape(groups, -1), position, 0, keepdims=False)
    coeffs = unit_inverse(own_units, step_count)

    wide_source = with_halo(source, (("lat", 3),), width)
    wide_start = with_halo(warm_start, (("lat", 3),), width)
    wide_depth = with_halo(depth, (("lat", 0),), width)
    global_row = lat_pos * rows - width + jnp.arange(rows + 2 * width, dtype=jnp.int32)
    row_mask = ((global_row >= 0) & (global_row < rows * lat_count)).astype(jnp.float32)
    solved = chebyshev(wide_source, wide_start, wide_depth, coeffs, row_mask[:, None])
    solved = solved[:, :, :, width : width + rows]
    spectrum = jnp.where(own_filled[:, None, None, None, None], solved, 0.0)

    solved_cols = from_owners(solved)
    corr = jnp.einsum(
        "sfpyx,tsp->fyxt", solved_cols, inverse_table, precision=lax.Precision.HIGHEST
    )
    updated = state_cols + corr
    return (updated, spectrum)


def solution(mesh):
    return jax.shard_map(
        body,
        mesh=mesh,
        in_specs=(
            P("tm", None, "lat", None),
            P("tm", None, "lat", None),
            P(None, "lat", None),
            P("lat", None),
            P("tm", None, None, "lat", None),
            P(),
            P(),
        ),
        out_specs=(P(None, "lat", "tm", None), P("tm", None, None, "lat", None)),
        check_vma=False,
    )
```

```python
import math

import jax
import jax.numpy as jnp
from jax import lax
from jax.sharding import Mesh
from jax.sharding import PartitionSpec as P

SWEEPS = 6
TM = ("ty", "tx")


HALF_COUPLING = 0.125
CORIOLIS = 0.2
FRICTION = 1.0
ALPHA = 0.1
SPREAD = 0.2


def with_halo(cells, sides, width):
    for axis, dim in sides:
        count = lax.axis_size(axis)
        ends = count - 1
        head = lax.slice_in_dim(cells, 0, width, axis=dim)
        tail = lax.slice_in_dim(cells, cells.shape[dim] - width, cells.shape[dim], axis=dim)
        cells = jnp.concatenate(
            [
                lax.ppermute(tail, axis, [(i, (i + 1) % count) for i in range(ends)]),
                cells,
                lax.ppermute(head, axis, [((i + 1) % count, i) for i in range(ends)]),
            ],
            axis=dim,
        )
    return cells


def shifted(value, axis, by):
    size = lax.axis_size(axis)
    pairs = [(i, i + by) for i in range(size) if 0 <= i + by < size]
    return lax.ppermute(value, axis, pairs)


def flux_operator(state, depth, pad_rule, row_mask=None):
    height = state[..., 0:1, :, :, :]
    east = state[..., 1:2, :, :, :]
    north = state[..., 2:3, :, :, :]
    if row_mask is not None:
        height = height * row_mask
    flux = jnp.concatenate([height, depth * east, depth * north], axis=-4)
    padded = pad_rule(flux)
    grad_x = padded[..., 0:1, :, 1:-1, 2:] - padded[..., 0:1, :, 1:-1, :-2]
    grad_y = padded[..., 0:1, :, 2:, 1:-1] - padded[..., 0:1, :, :-2, 1:-1]
    diverge = (
        padded[..., 1:2, :, 1:-1, 2:]
        - padded[..., 1:2, :, 1:-1, :-2]
        + (padded[..., 2:3, :, 2:, 1:-1] - padded[..., 2:3, :, :-2, 1:-1])
    )
    new_height = HALF_COUPLING * diverge
    new_east = HALF_COUPLING * grad_x - CORIOLIS * north
    new_north = HALF_COUPLING * grad_y + CORIOLIS * east
    return jnp.concatenate([new_height, new_east, new_north], axis=-4)


def row_rims(flux):
    rows_done = with_halo(flux, (("lat", 3),), 1)
    return jnp.pad(rows_done, ((0, 0), (0, 0), (0, 0), (0, 0), (1, 1)))


def zero_rim(values):
    widths = [(0, 0)] * (values.ndim - 2) + [(1, 1), (1, 1)]
    return jnp.pad(values, widths)


def all_to_all(x, split_axis, concat_axis):
    n_out, n_in = lax.axis_size("ty"), lax.axis_size("tx")
    shape = x.shape
    size = shape[split_axis]
    x = x.reshape(
        shape[:split_axis] + (n_out, n_in, size // (n_out * n_in)) + shape[split_axis + 1 :]
    )
    x = lax.all_to_all(x, "tx", split_axis + 1, 0, tiled=False)
    x = lax.all_to_all(x, "ty", split_axis + 1, 0, tiled=False)
    x = x.reshape((n_out * n_in,) + x.shape[2:])
    x = jnp.moveaxis(x, 0, concat_axis)
    s = x.shape
    return x.reshape(s[:concat_axis] + (s[concat_axis] * s[concat_axis + 1],) + s[concat_axis + 2 :])


def to_owners(slots):
    return all_to_all(slots, 0, 4)


def from_owners(slots):
    return all_to_all(slots, 4, 0)


def slot_tables(units, filled, step_count):
    index_t = jnp.arange(step_count, dtype=jnp.int32)
    phases = index_t[:, None] * units[None, :] % step_count
    angles = phases.astype(jnp.float32) * (2.0 * math.pi / step_count)
    cosine = jnp.cos(angles)
    sine = jnp.sin(angles)
    parity = (1 - 2 * (index_t % 2)).astype(jnp.float32)
    first = units == 0
    times = index_t.astype(jnp.float32) / step_count
    damping = jnp.exp(times * math.log(ALPHA)) / math.sqrt(step_count)
    growth = jnp.exp(-times * math.log(ALPHA)) / math.sqrt(step_count)
    forward_imag = jnp.where(first[None, :], parity[:, None], -sine)
    forward_table = jnp.stack([cosine, forward_imag], axis=2) * damping[:, None, None]
    weights = jnp.where(first, 1.0, 2.0).astype(jnp.float32)
    inverse_real = cosine * weights[None, :]
    inverse_imag = jnp.where(first[None, :], parity[:, None], -2.0 * sine)
    keep = filled.astype(jnp.float32)[None, :, None]
    inverse_table = jnp.stack([inverse_real, inverse_imag], axis=2) * growth[:, None, None] * keep
    return (forward_table, inverse_table)


def unit_inverse(pair_ids, step_count):
    angles = pair_ids.astype(jnp.float32) * (2.0 * math.pi / step_count)
    ratio = math.exp(math.log(ALPHA) / step_count)
    real_shift = 1.0 + FRICTION - ratio * jnp.cos(angles)
    imag_shift = ratio * jnp.sin(angles)
    denominator = real_shift * real_shift + imag_shift * imag_shift
    real_inv = real_shift / denominator
    imag_inv = -imag_shift / denominator
    is_first = pair_ids == 0
    upper_left = jnp.where(is_first, 1.0 / (1.0 + FRICTION - ratio), real_inv)
    upper_right = jnp.where(is_first, 0.0, -imag_inv)
    lower_left = jnp.where(is_first, 0.0, imag_inv)
    lower_right = jnp.where(is_first, 1.0 / (1.0 + FRICTION + ratio), real_inv)
    return (upper_left, upper_right, lower_left, lower_right)


def apply_inverse(coeffs, values):
    shaped = [c[:, None, None, None] for c in coeffs]
    real_part = values[:, :, 0]
    imag_part = values[:, :, 1]
    new_real = shaped[0] * real_part + shaped[1] * imag_part
    new_imag = shaped[2] * real_part + shaped[3] * imag_part
    return jnp.stack([new_real, new_imag], axis=2)


def chebyshev(source, start, depth, coeffs, row_mask):
    iterate = start
    for sweep in range(SWEEPS):
        weight = 1.0 / (1.0 + SPREAD * math.cos(math.pi * (2 * sweep + 1) / (2 * SWEEPS)))
        flux = flux_operator(iterate, depth, zero_rim, row_mask)
        update = apply_inverse(coeffs, source - flux) - iterate
        iterate = iterate + weight * update
    return iterate


def body(trajectory, forcing, initial_state, depth, warm_start, slot_unit, unit_count):
    groups = lax.axis_size("ty") * lax.axis_size("tx")
    position = lax.axis_index("ty") * lax.axis_size("tx") + lax.axis_index("tx")
    local_steps = trajectory.shape[0]
    step_count = local_steps * groups
    rows = depth.shape[0]
    lat_count = lax.axis_size("lat")
    lat_pos = lax.axis_index("lat")
    width = 8 * ((SWEEPS + 7) // 8)

    last_step = shifted(trajectory[local_steps - 1], TM, 1)
    first_previous = jnp.where(position == 0, initial_state, last_step)
    previous = jnp.concatenate([first_previous[None], trajectory[: local_steps - 1]], axis=0)
    flux_term = flux_operator(trajectory[:, :, None], depth, row_rims)[:, :, 0]
    resid = forcing - ((1.0 + FRICTION) * trajectory - previous + flux_term)
    moved = all_to_all(jnp.stack([trajectory, resid], axis=1), 4, 0)
    moved_state, moved_resid = moved[:, 0], moved[:, 1]
    state_cols = jnp.transpose(moved_state, (1, 2, 3, 0))
    fields, col_count = moved_resid.shape[1], moved_resid.shape[3]

    flat_units = slot_unit.reshape(-1)
    slot_total = slot_unit.shape[1]
    filled = (jnp.arange(slot_total, dtype=jnp.int32)[None, :] < unit_count[:, None]).reshape(-1)
    forward_table, inverse_table = slot_tables(flat_units, filled, step_count)

    outgoing = jnp.einsum(
        "tsp,tfyx->sfpyx", forward_table, moved_resid, precision=lax.Precision.HIGHEST
    )
    source = to_owners(outgoing)

    own_units = lax.dynamic_index_in_dim(slot_unit, position, 0, keepdims=False)
    own_filled = lax.dynamic_index_in_dim(filled.reshape(groups, -1), position, 0, keepdims=False)
    coeffs = unit_inverse(own_units, step_count)

    wide_source = with_halo(source, (("lat", 3),), width)
    wide_start = with_halo(warm_start, (("lat", 3),), width)
    wide_depth = with_halo(depth, (("lat", 0),), width)
    global_row = lat_pos * rows - width + jnp.arange(rows + 2 * width, dtype=jnp.int32)
    row_mask = ((global_row >= 0) & (global_row < rows * lat_count)).astype(jnp.float32)
    solved = chebyshev(wide_source, wide_start, wide_depth, coeffs, row_mask[:, None])
    solved = solved[:, :, :, width : width + rows]
    spectrum = jnp.where(own_filled[:, None, None, None, None], solved, 0.0)

    solved_cols = from_owners(solved)
    corr = jnp.einsum(
        "sfpyx,tsp->fyxt", solved_cols, inverse_table, precision=lax.Precision.HIGHEST
    )
    updated = state_cols + corr
    return (updated, spectrum)


def solution(mesh):
    tm_size, lat_size = mesh.shape["tm"], mesh.shape["lat"]
    inner = math.gcd(tm_size, 8)
    split = Mesh(mesh.devices.reshape(tm_size // inner, inner, lat_size), ("ty", "tx", "lat"))
    return jax.shard_map(
        body,
        mesh=split,
        in_specs=(
            P(TM, None, "lat", None),
            P(TM, None, "lat", None),
            P(None, "lat", None),
            P("lat", None),
            P(TM, None, None, "lat", None),
            P(),
            P(),
        ),
        out_specs=(P(None, "lat", TM, None), P(TM, None, None, "lat", None)),
        check_vma=False,
    )
```

```python
import math

import jax
import jax.numpy as jnp
from jax import lax
from jax.sharding import PartitionSpec as P

SWEEPS = 6


HALF_COUPLING = 0.125
CORIOLIS = 0.2
FRICTION = 1.0
ALPHA = 0.1
SPREAD = 0.2


def with_halo(cells, sides, width):
    for axis, dim in sides:
        count = lax.axis_size(axis)
        ends = count - 1
        head = lax.slice_in_dim(cells, 0, width, axis=dim)
        tail = lax.slice_in_dim(cells, cells.shape[dim] - width, cells.shape[dim], axis=dim)
        cells = jnp.concatenate(
            [
                lax.ppermute(tail, axis, [(i, (i + 1) % count) for i in range(ends)]),
                cells,
                lax.ppermute(head, axis, [((i + 1) % count, i) for i in range(ends)]),
            ],
            axis=dim,
        )
    return cells


def shifted(value, axis, by):
    size = lax.axis_size(axis)
    pairs = [(i, i + by) for i in range(size) if 0 <= i + by < size]
    return lax.ppermute(value, axis, pairs)


def flux_operator(state, depth, pad_rule, row_mask=None):
    height = state[..., 0:1, :, :, :]
    east = state[..., 1:2, :, :, :]
    north = state[..., 2:3, :, :, :]
    if row_mask is not None:
        height = height * row_mask
    flux = jnp.concatenate([height, depth * east, depth * north], axis=-4)
    padded = pad_rule(flux)
    grad_x = padded[..., 0:1, :, 1:-1, 2:] - padded[..., 0:1, :, 1:-1, :-2]
    grad_y = padded[..., 0:1, :, 2:, 1:-1] - padded[..., 0:1, :, :-2, 1:-1]
    diverge = (
        padded[..., 1:2, :, 1:-1, 2:]
        - padded[..., 1:2, :, 1:-1, :-2]
        + (padded[..., 2:3, :, 2:, 1:-1] - padded[..., 2:3, :, :-2, 1:-1])
    )
    new_height = HALF_COUPLING * diverge
    new_east = HALF_COUPLING * grad_x - CORIOLIS * north
    new_north = HALF_COUPLING * grad_y + CORIOLIS * east
    return jnp.concatenate([new_height, new_east, new_north], axis=-4)


def row_rims(flux):
    rows_done = with_halo(flux, (("lat", 3),), 1)
    return jnp.pad(rows_done, ((0, 0), (0, 0), (0, 0), (0, 0), (1, 1)))


def zero_rim(values):
    widths = [(0, 0)] * (values.ndim - 2) + [(1, 1), (1, 1)]
    return jnp.pad(values, widths)


def to_owners(slots):
    return lax.all_to_all(slots, "tm", split_axis=0, concat_axis=4, tiled=True)


def from_owners(slots):
    return lax.all_to_all(slots, "tm", split_axis=4, concat_axis=0, tiled=True)


def slot_tables(units, filled, step_count):
    index_t = jnp.arange(step_count, dtype=jnp.int32)
    phases = index_t[:, None] * units[None, :] % step_count
    angles = phases.astype(jnp.float32) * (2.0 * math.pi / step_count)
    cosine = jnp.cos(angles)
    sine = jnp.sin(angles)
    parity = (1 - 2 * (index_t % 2)).astype(jnp.float32)
    first = units == 0
    times = index_t.astype(jnp.float32) / step_count
    damping = jnp.exp(times * math.log(ALPHA)) / math.sqrt(step_count)
    growth = jnp.exp(-times * math.log(ALPHA)) / math.sqrt(step_count)
    forward_imag = jnp.where(first[None, :], parity[:, None], -sine)
    forward_table = jnp.stack([cosine, forward_imag], axis=2) * damping[:, None, None]
    weights = jnp.where(first, 1.0, 2.0).astype(jnp.float32)
    inverse_real = cosine * weights[None, :]
    inverse_imag = jnp.where(first[None, :], parity[:, None], -2.0 * sine)
    keep = filled.astype(jnp.float32)[None, :, None]
    inverse_table = jnp.stack([inverse_real, inverse_imag], axis=2) * growth[:, None, None] * keep
    return (forward_table, inverse_table)


def unit_inverse(pair_ids, step_count):
    angles = pair_ids.astype(jnp.float32) * (2.0 * math.pi / step_count)
    ratio = math.exp(math.log(ALPHA) / step_count)
    real_shift = 1.0 + FRICTION - ratio * jnp.cos(angles)
    imag_shift = ratio * jnp.sin(angles)
    denominator = real_shift * real_shift + imag_shift * imag_shift
    real_inv = real_shift / denominator
    imag_inv = -imag_shift / denominator
    is_first = pair_ids == 0
    upper_left = jnp.where(is_first, 1.0 / (1.0 + FRICTION - ratio), real_inv)
    upper_right = jnp.where(is_first, 0.0, -imag_inv)
    lower_left = jnp.where(is_first, 0.0, imag_inv)
    lower_right = jnp.where(is_first, 1.0 / (1.0 + FRICTION + ratio), real_inv)
    return (upper_left, upper_right, lower_left, lower_right)


def apply_inverse(coeffs, values):
    shaped = [c[:, None, None, None] for c in coeffs]
    real_part = values[:, :, 0]
    imag_part = values[:, :, 1]
    new_real = shaped[0] * real_part + shaped[1] * imag_part
    new_imag = shaped[2] * real_part + shaped[3] * imag_part
    return jnp.stack([new_real, new_imag], axis=2)


def chebyshev(source, start, depth, coeffs, row_mask):
    iterate = start
    for sweep in range(SWEEPS):
        weight = 1.0 / (1.0 + SPREAD * math.cos(math.pi * (2 * sweep + 1) / (2 * SWEEPS)))
        flux = flux_operator(iterate, depth, zero_rim, row_mask)
        update = apply_inverse(coeffs, source - flux) - iterate
        iterate = iterate + weight * update
    return iterate


def lat_halo(arrays, width):
    flat = [a.reshape((-1,) + a.shape[-2:]) for a in arrays]
    packed = jnp.concatenate(flat, axis=0)
    rows = packed.shape[1]
    count = lax.axis_size("lat")
    above = lax.ppermute(packed[:, rows - width :], "lat", [(i, i + 1) for i in range(count - 1)])
    below = lax.ppermute(packed[:, :width], "lat", [(i + 1, i) for i in range(count - 1)])
    wide = jnp.concatenate([above, packed, below], axis=1)
    out, offset = [], 0
    for a, f in zip(arrays, flat):
        piece = wide[offset : offset + f.shape[0]]
        out.append(piece.reshape(a.shape[:-2] + piece.shape[1:]))
        offset += f.shape[0]
    return out


def body(trajectory, forcing, initial_state, depth, warm_start, slot_unit, unit_count):
    groups = lax.axis_size("tm")
    position = lax.axis_index("tm")
    local_steps = trajectory.shape[0]
    step_count = local_steps * groups
    rows = depth.shape[0]
    lat_count = lax.axis_size("lat")
    lat_pos = lax.axis_index("lat")
    width = 8 * ((SWEEPS + 7) // 8)

    wide_traj, wide_forcing, wide_initial, wide_depth, wide_start = lat_halo(
        [trajectory, forcing, initial_state, depth, warm_start], width
    )
    flux_term = flux_operator(wide_traj[:, :, None], wide_depth, zero_rim)[:, :, 0]
    partial = wide_forcing - ((1.0 + FRICTION) * wide_traj + flux_term)
    moved = lax.all_to_all(
        jnp.stack([wide_traj, partial], axis=1), "tm", split_axis=4, concat_axis=0, tiled=True
    )
    traj_cols, partial_cols = moved[:, 0], moved[:, 1]
    col_count = traj_cols.shape[3]
    initial_cols = lax.dynamic_slice_in_dim(wide_initial, position * col_count, col_count, axis=2)
    previous = jnp.concatenate([initial_cols[None], traj_cols[:-1]], axis=0)
    resid_cols = partial_cols + previous
    state_cols = jnp.transpose(traj_cols[:, :, width : width + rows], (1, 2, 3, 0))

    flat_units = slot_unit.reshape(-1)
    slot_total = slot_unit.shape[1]
    filled = (jnp.arange(slot_total, dtype=jnp.int32)[None, :] < unit_count[:, None]).reshape(-1)
    forward_table, inverse_table = slot_tables(flat_units, filled, step_count)

    outgoing = jnp.einsum(
        "tsp,tfyx->sfpyx", forward_table, resid_cols, precision=lax.Precision.HIGHEST
    )
    wide_source = to_owners(outgoing)

    own_units = lax.dynamic_index_in_dim(slot_unit, position, 0, keepdims=False)
    own_filled = lax.dynamic_index_in_dim(filled.reshape(groups, -1), position, 0, keepdims=False)
    coeffs = unit_inverse(own_units, step_count)

    global_row = lat_pos * rows - width + jnp.arange(rows + 2 * width, dtype=jnp.int32)
    row_mask = ((global_row >= 0) & (global_row < rows * lat_count)).astype(jnp.float32)
    solved = chebyshev(wide_source, wide_start, wide_depth, coeffs, row_mask[:, None])
    solved = solved[:, :, :, width : width + rows]
    spectrum = jnp.where(own_filled[:, None, None, None, None], solved, 0.0)

    solved_cols = from_owners(solved)
    corr = jnp.einsum(
        "sfpyx,tsp->fyxt", solved_cols, inverse_table, precision=lax.Precision.HIGHEST
    )
    updated = state_cols + corr
    return (updated, spectrum)


def solution(mesh):
    return jax.shard_map(
        body,
        mesh=mesh,
        in_specs=(
            P("tm", None, "lat", None),
            P("tm", None, "lat", None),
            P(None, "lat", None),
            P("lat", None),
            P("tm", None, None, "lat", None),
            P(),
            P(),
        ),
        out_specs=(P(None, "lat", "tm", None), P("tm", None, None, "lat", None)),
        check_vma=False,
    )
```

```python
import math

import jax
import jax.numpy as jnp
from jax import lax
from jax.sharding import PartitionSpec as P

SWEEPS = 6


HALF_COUPLING = 0.125
CORIOLIS = 0.2
FRICTION = 1.0
ALPHA = 0.1
SPREAD = 0.2


def with_halo(cells, sides, width):
    for axis, dim in sides:
        count = lax.axis_size(axis)
        ends = count - 1
        head = lax.slice_in_dim(cells, 0, width, axis=dim)
        tail = lax.slice_in_dim(cells, cells.shape[dim] - width, cells.shape[dim], axis=dim)
        cells = jnp.concatenate(
            [
                lax.ppermute(tail, axis, [(i, (i + 1) % count) for i in range(ends)]),
                cells,
                lax.ppermute(head, axis, [((i + 1) % count, i) for i in range(ends)]),
            ],
            axis=dim,
        )
    return cells


def shifted(value, axis, by):
    size = lax.axis_size(axis)
    pairs = [(i, i + by) for i in range(size) if 0 <= i + by < size]
    return lax.ppermute(value, axis, pairs)


def flux_operator(state, depth, pad_rule, row_mask=None):
    height = state[..., 0:1, :, :, :]
    east = state[..., 1:2, :, :, :]
    north = state[..., 2:3, :, :, :]
    if row_mask is not None:
        height = height * row_mask
    flux = jnp.concatenate([height, depth * east, depth * north], axis=-4)
    padded = pad_rule(flux)
    grad_x = padded[..., 0:1, :, 1:-1, 2:] - padded[..., 0:1, :, 1:-1, :-2]
    grad_y = padded[..., 0:1, :, 2:, 1:-1] - padded[..., 0:1, :, :-2, 1:-1]
    diverge = (
        padded[..., 1:2, :, 1:-1, 2:]
        - padded[..., 1:2, :, 1:-1, :-2]
        + (padded[..., 2:3, :, 2:, 1:-1] - padded[..., 2:3, :, :-2, 1:-1])
    )
    new_height = HALF_COUPLING * diverge
    new_east = HALF_COUPLING * grad_x - CORIOLIS * north
    new_north = HALF_COUPLING * grad_y + CORIOLIS * east
    return jnp.concatenate([new_height, new_east, new_north], axis=-4)


def row_rims(flux):
    rows_done = with_halo(flux, (("lat", 3),), 1)
    return jnp.pad(rows_done, ((0, 0), (0, 0), (0, 0), (0, 0), (1, 1)))


def zero_rim(values):
    widths = [(0, 0)] * (values.ndim - 2) + [(1, 1), (1, 1)]
    return jnp.pad(values, widths)


def to_owners(slots):
    return lax.all_to_all(slots, "tm", split_axis=0, concat_axis=4, tiled=True)


def from_owners(slots):
    return lax.all_to_all(slots, "tm", split_axis=4, concat_axis=0, tiled=True)


def slot_tables(units, filled, step_count):
    index_t = jnp.arange(step_count, dtype=jnp.int32)
    phases = index_t[:, None] * units[None, :] % step_count
    angles = phases.astype(jnp.float32) * (2.0 * math.pi / step_count)
    cosine = jnp.cos(angles)
    sine = jnp.sin(angles)
    parity = (1 - 2 * (index_t % 2)).astype(jnp.float32)
    first = units == 0
    times = index_t.astype(jnp.float32) / step_count
    damping = jnp.exp(times * math.log(ALPHA)) / math.sqrt(step_count)
    growth = jnp.exp(-times * math.log(ALPHA)) / math.sqrt(step_count)
    forward_imag = jnp.where(first[None, :], parity[:, None], -sine)
    forward_table = jnp.stack([cosine, forward_imag], axis=2) * damping[:, None, None]
    weights = jnp.where(first, 1.0, 2.0).astype(jnp.float32)
    inverse_real = cosine * weights[None, :]
    inverse_imag = jnp.where(first[None, :], parity[:, None], -2.0 * sine)
    keep = filled.astype(jnp.float32)[None, :, None]
    inverse_table = jnp.stack([inverse_real, inverse_imag], axis=2) * growth[:, None, None] * keep
    return (forward_table, inverse_table)


def unit_inverse(pair_ids, step_count):
    angles = pair_ids.astype(jnp.float32) * (2.0 * math.pi / step_count)
    ratio = math.exp(math.log(ALPHA) / step_count)
    real_shift = 1.0 + FRICTION - ratio * jnp.cos(angles)
    imag_shift = ratio * jnp.sin(angles)
    denominator = real_shift * real_shift + imag_shift * imag_shift
    real_inv = real_shift / denominator
    imag_inv = -imag_shift / denominator
    is_first = pair_ids == 0
    upper_left = jnp.where(is_first, 1.0 / (1.0 + FRICTION - ratio), real_inv)
    upper_right = jnp.where(is_first, 0.0, -imag_inv)
    lower_left = jnp.where(is_first, 0.0, imag_inv)
    lower_right = jnp.where(is_first, 1.0 / (1.0 + FRICTION + ratio), real_inv)
    return (upper_left, upper_right, lower_left, lower_right)


def apply_inverse(coeffs, values):
    shaped = [c[:, None, None, None] for c in coeffs]
    real_part = values[:, :, 0]
    imag_part = values[:, :, 1]
    new_real = shaped[0] * real_part + shaped[1] * imag_part
    new_imag = shaped[2] * real_part + shaped[3] * imag_part
    return jnp.stack([new_real, new_imag], axis=2)


def chebyshev(source, start, depth, coeffs, row_mask):
    iterate = start
    for sweep in range(SWEEPS):
        weight = 1.0 / (1.0 + SPREAD * math.cos(math.pi * (2 * sweep + 1) / (2 * SWEEPS)))
        flux = flux_operator(iterate, depth, zero_rim, row_mask)
        update = apply_inverse(coeffs, source - flux) - iterate
        iterate = iterate + weight * update
    return iterate


def lat_halo(arrays, width):
    flat = [a.reshape((-1,) + a.shape[-2:]) for a in arrays]
    packed = jnp.concatenate(flat, axis=0)
    rows = packed.shape[1]
    count = lax.axis_size("lat")
    above = lax.ppermute(packed[:, rows - width :], "lat", [(i, i + 1) for i in range(count - 1)])
    below = lax.ppermute(packed[:, :width], "lat", [(i + 1, i) for i in range(count - 1)])
    wide = jnp.concatenate([above, packed, below], axis=1)
    out, offset = [], 0
    for a, f in zip(arrays, flat):
        piece = wide[offset : offset + f.shape[0]]
        out.append(piece.reshape(a.shape[:-2] + piece.shape[1:]))
        offset += f.shape[0]
    return out


def body(trajectory, forcing, initial_state, depth, warm_start, slot_unit, unit_count):
    groups = lax.axis_size("tm")
    position = lax.axis_index("tm")
    local_steps = trajectory.shape[0]
    step_count = local_steps * groups
    rows = depth.shape[0]
    lat_count = lax.axis_size("lat")
    lat_pos = lax.axis_index("lat")
    width = 8 * ((SWEEPS + 7) // 8)

    wide_traj, wide_forcing, wide_initial, wide_depth, wide_start = lat_halo(
        [trajectory, forcing, initial_state, depth, warm_start], width
    )
    flux_term = flux_operator(wide_traj[:, :, None], wide_depth, zero_rim)[:, :, 0]
    partial = wide_forcing - ((1.0 + FRICTION) * wide_traj + flux_term)
    keep = width - SWEEPS + 1
    band = slice(keep, rows + 2 * width - keep)
    moved = lax.all_to_all(
        jnp.stack([wide_traj[:, :, band], partial[:, :, band]], axis=1),
        "tm",
        split_axis=4,
        concat_axis=0,
        tiled=True,
    )
    traj_cols, partial_cols = moved[:, 0], moved[:, 1]
    col_count = traj_cols.shape[3]
    initial_cols = lax.dynamic_slice_in_dim(
        wide_initial[:, band], position * col_count, col_count, axis=2
    )
    previous = jnp.concatenate([initial_cols[None], traj_cols[:-1]], axis=0)
    resid_cols = partial_cols + previous
    inner = width - keep
    state_cols = jnp.transpose(traj_cols[:, :, inner : inner + rows], (1, 2, 3, 0))

    flat_units = slot_unit.reshape(-1)
    slot_total = slot_unit.shape[1]
    filled = (jnp.arange(slot_total, dtype=jnp.int32)[None, :] < unit_count[:, None]).reshape(-1)
    forward_table, inverse_table = slot_tables(flat_units, filled, step_count)

    outgoing = jnp.einsum(
        "tsp,tfyx->sfpyx", forward_table, resid_cols, precision=lax.Precision.HIGHEST
    )
    pads = ((0, 0), (0, 0), (0, 0), (keep, keep), (0, 0))
    wide_source = jnp.pad(to_owners(outgoing), pads)

    own_units = lax.dynamic_index_in_dim(slot_unit, position, 0, keepdims=False)
    own_filled = lax.dynamic_index_in_dim(filled.reshape(groups, -1), position, 0, keepdims=False)
    coeffs = unit_inverse(own_units, step_count)

    global_row = lat_pos * rows - width + jnp.arange(rows + 2 * width, dtype=jnp.int32)
    row_mask = ((global_row >= 0) & (global_row < rows * lat_count)).astype(jnp.float32)
    solved = chebyshev(wide_source, wide_start, wide_depth, coeffs, row_mask[:, None])
    solved = solved[:, :, :, width : width + rows]
    spectrum = jnp.where(own_filled[:, None, None, None, None], solved, 0.0)

    solved_cols = from_owners(solved)
    corr = jnp.einsum(
        "sfpyx,tsp->fyxt", solved_cols, inverse_table, precision=lax.Precision.HIGHEST
    )
    updated = state_cols + corr
    return (updated, spectrum)


def solution(mesh):
    return jax.shard_map(
        body,
        mesh=mesh,
        in_specs=(
            P("tm", None, "lat", None),
            P("tm", None, "lat", None),
            P(None, "lat", None),
            P("lat", None),
            P("tm", None, None, "lat", None),
            P(),
            P(),
        ),
        out_specs=(P(None, "lat", "tm", None), P("tm", None, None, "lat", None)),
        check_vma=False,
    )
```

```python
import math

import jax
import jax.numpy as jnp
from jax import lax
from jax.sharding import PartitionSpec as P

SWEEPS = 6


HALF_COUPLING = 0.125
CORIOLIS = 0.2
FRICTION = 1.0
ALPHA = 0.1
SPREAD = 0.2


def with_halo(cells, sides, width):
    for axis, dim in sides:
        count = lax.axis_size(axis)
        ends = count - 1
        head = lax.slice_in_dim(cells, 0, width, axis=dim)
        tail = lax.slice_in_dim(cells, cells.shape[dim] - width, cells.shape[dim], axis=dim)
        cells = jnp.concatenate(
            [
                lax.ppermute(tail, axis, [(i, (i + 1) % count) for i in range(ends)]),
                cells,
                lax.ppermute(head, axis, [((i + 1) % count, i) for i in range(ends)]),
            ],
            axis=dim,
        )
    return cells


def shifted(value, axis, by):
    size = lax.axis_size(axis)
    pairs = [(i, i + by) for i in range(size) if 0 <= i + by < size]
    return lax.ppermute(value, axis, pairs)


def flux_operator(state, depth, pad_rule, row_mask=None):
    height = state[..., 0:1, :, :, :]
    east = state[..., 1:2, :, :, :]
    north = state[..., 2:3, :, :, :]
    if row_mask is not None:
        height = height * row_mask
    flux = jnp.concatenate([height, depth * east, depth * north], axis=-4)
    padded = pad_rule(flux)
    grad_x = padded[..., 0:1, :, 1:-1, 2:] - padded[..., 0:1, :, 1:-1, :-2]
    grad_y = padded[..., 0:1, :, 2:, 1:-1] - padded[..., 0:1, :, :-2, 1:-1]
    diverge = (
        padded[..., 1:2, :, 1:-1, 2:]
        - padded[..., 1:2, :, 1:-1, :-2]
        + (padded[..., 2:3, :, 2:, 1:-1] - padded[..., 2:3, :, :-2, 1:-1])
    )
    new_height = HALF_COUPLING * diverge
    new_east = HALF_COUPLING * grad_x - CORIOLIS * north
    new_north = HALF_COUPLING * grad_y + CORIOLIS * east
    return jnp.concatenate([new_height, new_east, new_north], axis=-4)


def row_rims(flux):
    rows_done = with_halo(flux, (("lat", 3),), 1)
    return jnp.pad(rows_done, ((0, 0), (0, 0), (0, 0), (0, 0), (1, 1)))


def zero_rim(values):
    widths = [(0, 0)] * (values.ndim - 2) + [(1, 1), (1, 1)]
    return jnp.pad(values, widths)


def to_owners(slots):
    return lax.all_to_all(slots, "tm", split_axis=0, concat_axis=4, tiled=True)


def from_owners(slots):
    return lax.all_to_all(slots, "tm", split_axis=4, concat_axis=0, tiled=True)


def slot_tables(units, filled, step_count):
    index_t = jnp.arange(step_count, dtype=jnp.int32)
    phases = index_t[:, None] * units[None, :] % step_count
    angles = phases.astype(jnp.float32) * (2.0 * math.pi / step_count)
    cosine = jnp.cos(angles)
    sine = jnp.sin(angles)
    parity = (1 - 2 * (index_t % 2)).astype(jnp.float32)
    first = units == 0
    times = index_t.astype(jnp.float32) / step_count
    damping = jnp.exp(times * math.log(ALPHA)) / math.sqrt(step_count)
    growth = jnp.exp(-times * math.log(ALPHA)) / math.sqrt(step_count)
    forward_imag = jnp.where(first[None, :], parity[:, None], -sine)
    forward_table = jnp.stack([cosine, forward_imag], axis=2) * damping[:, None, None]
    weights = jnp.where(first, 1.0, 2.0).astype(jnp.float32)
    inverse_real = cosine * weights[None, :]
    inverse_imag = jnp.where(first[None, :], parity[:, None], -2.0 * sine)
    keep = filled.astype(jnp.float32)[None, :, None]
    inverse_table = jnp.stack([inverse_real, inverse_imag], axis=2) * growth[:, None, None] * keep
    return (forward_table, inverse_table)


def unit_inverse(pair_ids, step_count):
    angles = pair_ids.astype(jnp.float32) * (2.0 * math.pi / step_count)
    ratio = math.exp(math.log(ALPHA) / step_count)
    real_shift = 1.0 + FRICTION - ratio * jnp.cos(angles)
    imag_shift = ratio * jnp.sin(angles)
    denominator = real_shift * real_shift + imag_shift * imag_shift
    real_inv = real_shift / denominator
    imag_inv = -imag_shift / denominator
    is_first = pair_ids == 0
    upper_left = jnp.where(is_first, 1.0 / (1.0 + FRICTION - ratio), real_inv)
    upper_right = jnp.where(is_first, 0.0, -imag_inv)
    lower_left = jnp.where(is_first, 0.0, imag_inv)
    lower_right = jnp.where(is_first, 1.0 / (1.0 + FRICTION + ratio), real_inv)
    return (upper_left, upper_right, lower_left, lower_right)


def apply_inverse(coeffs, values):
    shaped = [c[:, None, None, None] for c in coeffs]
    real_part = values[:, :, 0]
    imag_part = values[:, :, 1]
    new_real = shaped[0] * real_part + shaped[1] * imag_part
    new_imag = shaped[2] * real_part + shaped[3] * imag_part
    return jnp.stack([new_real, new_imag], axis=2)


def chebyshev(source, start, depth, coeffs, row_mask):
    iterate = start
    for sweep in range(SWEEPS):
        weight = 1.0 / (1.0 + SPREAD * math.cos(math.pi * (2 * sweep + 1) / (2 * SWEEPS)))
        flux = flux_operator(iterate, depth, zero_rim, row_mask)
        update = apply_inverse(coeffs, source - flux) - iterate
        iterate = iterate + weight * update
    return iterate


def lat_halo(arrays, width):
    flat = [a.reshape((-1,) + a.shape[-2:]) for a in arrays]
    packed = jnp.concatenate(flat, axis=0)
    rows = packed.shape[1]
    count = lax.axis_size("lat")
    above = lax.ppermute(packed[:, rows - width :], "lat", [(i, i + 1) for i in range(count - 1)])
    below = lax.ppermute(packed[:, :width], "lat", [(i + 1, i) for i in range(count - 1)])
    wide = jnp.concatenate([above, packed, below], axis=1)
    out, offset = [], 0
    for a, f in zip(arrays, flat):
        piece = wide[offset : offset + f.shape[0]]
        out.append(piece.reshape(a.shape[:-2] + piece.shape[1:]))
        offset += f.shape[0]
    return out


def body(trajectory, forcing, initial_state, depth, warm_start, slot_unit, unit_count):
    groups = lax.axis_size("tm")
    position = lax.axis_index("tm")
    local_steps = trajectory.shape[0]
    step_count = local_steps * groups
    rows = depth.shape[0]
    lat_count = lax.axis_size("lat")
    lat_pos = lax.axis_index("lat")
    width = 8 * ((SWEEPS + 7) // 8)

    wide_traj, wide_forcing, wide_initial, wide_depth, wide_start = lat_halo(
        [trajectory, forcing, initial_state, depth, warm_start], width
    )
    flux_term = flux_operator(wide_traj[:, :, None], wide_depth, zero_rim)[:, :, 0]
    partial = wide_forcing - ((1.0 + FRICTION) * wide_traj + flux_term)
    keep = width - SWEEPS + 1
    band = slice(keep, rows + 2 * width - keep)
    moved = lax.all_to_all(
        jnp.stack([wide_traj[:, :, band], partial[:, :, band]], axis=1),
        "tm",
        split_axis=4,
        concat_axis=0,
        tiled=True,
    )
    traj_cols, partial_cols = moved[:, 0], moved[:, 1]
    col_count = traj_cols.shape[3]
    initial_cols = lax.dynamic_slice_in_dim(
        wide_initial[:, band], position * col_count, col_count, axis=2
    )
    previous = jnp.concatenate([initial_cols[None], traj_cols[:-1]], axis=0)
    resid_cols = partial_cols + previous
    inner = width - keep
    state_cols = jnp.transpose(traj_cols[:, :, inner : inner + rows], (1, 2, 3, 0))

    flat_units = slot_unit.reshape(-1)
    slot_total = slot_unit.shape[1]
    filled = (jnp.arange(slot_total, dtype=jnp.int32)[None, :] < unit_count[:, None]).reshape(-1)
    forward_table, inverse_table = slot_tables(flat_units, filled, step_count)

    outgoing = jnp.einsum(
        "tsp,tfyx->sfpyx", forward_table, resid_cols, precision=lax.Precision.HIGH
    )
    pads = ((0, 0), (0, 0), (0, 0), (keep, keep), (0, 0))
    wide_source = jnp.pad(to_owners(outgoing), pads)

    own_units = lax.dynamic_index_in_dim(slot_unit, position, 0, keepdims=False)
    own_filled = lax.dynamic_index_in_dim(filled.reshape(groups, -1), position, 0, keepdims=False)
    coeffs = unit_inverse(own_units, step_count)

    global_row = lat_pos * rows - width + jnp.arange(rows + 2 * width, dtype=jnp.int32)
    row_mask = ((global_row >= 0) & (global_row < rows * lat_count)).astype(jnp.float32)
    solved = chebyshev(wide_source, wide_start, wide_depth, coeffs, row_mask[:, None])
    solved = solved[:, :, :, width : width + rows]
    spectrum = jnp.where(own_filled[:, None, None, None, None], solved, 0.0)

    solved_cols = from_owners(solved)
    corr = jnp.einsum(
        "sfpyx,tsp->fyxt", solved_cols, inverse_table, precision=lax.Precision.HIGH
    )
    updated = state_cols + corr
    return (updated, spectrum)


def solution(mesh):
    return jax.shard_map(
        body,
        mesh=mesh,
        in_specs=(
            P("tm", None, "lat", None),
            P("tm", None, "lat", None),
            P(None, "lat", None),
            P("lat", None),
            P("tm", None, None, "lat", None),
            P(),
            P(),
        ),
        out_specs=(P(None, "lat", "tm", None), P("tm", None, None, "lat", None)),
        check_vma=False,
    )
```

```python
import math

import jax
import jax.numpy as jnp
from jax import lax
from jax.sharding import PartitionSpec as P

SWEEPS = 6


HALF_COUPLING = 0.125
CORIOLIS = 0.2
FRICTION = 1.0
ALPHA = 0.1
SPREAD = 0.2


def with_halo(cells, sides, width):
    for axis, dim in sides:
        count = lax.axis_size(axis)
        ends = count - 1
        head = lax.slice_in_dim(cells, 0, width, axis=dim)
        tail = lax.slice_in_dim(cells, cells.shape[dim] - width, cells.shape[dim], axis=dim)
        cells = jnp.concatenate(
            [
                lax.ppermute(tail, axis, [(i, (i + 1) % count) for i in range(ends)]),
                cells,
                lax.ppermute(head, axis, [((i + 1) % count, i) for i in range(ends)]),
            ],
            axis=dim,
        )
    return cells


def shifted(value, axis, by):
    size = lax.axis_size(axis)
    pairs = [(i, i + by) for i in range(size) if 0 <= i + by < size]
    return lax.ppermute(value, axis, pairs)


def flux_operator(state, depth, pad_rule, row_mask=None):
    height = state[..., 0:1, :, :, :]
    east = state[..., 1:2, :, :, :]
    north = state[..., 2:3, :, :, :]
    if row_mask is not None:
        height = height * row_mask
    flux = jnp.concatenate([height, depth * east, depth * north], axis=-4)
    padded = pad_rule(flux)
    grad_x = padded[..., 0:1, :, 1:-1, 2:] - padded[..., 0:1, :, 1:-1, :-2]
    grad_y = padded[..., 0:1, :, 2:, 1:-1] - padded[..., 0:1, :, :-2, 1:-1]
    diverge = (
        padded[..., 1:2, :, 1:-1, 2:]
        - padded[..., 1:2, :, 1:-1, :-2]
        + (padded[..., 2:3, :, 2:, 1:-1] - padded[..., 2:3, :, :-2, 1:-1])
    )
    new_height = HALF_COUPLING * diverge
    new_east = HALF_COUPLING * grad_x - CORIOLIS * north
    new_north = HALF_COUPLING * grad_y + CORIOLIS * east
    return jnp.concatenate([new_height, new_east, new_north], axis=-4)


def row_rims(flux):
    rows_done = with_halo(flux, (("lat", 3),), 1)
    return jnp.pad(rows_done, ((0, 0), (0, 0), (0, 0), (0, 0), (1, 1)))


def zero_rim(values):
    widths = [(0, 0)] * (values.ndim - 2) + [(1, 1), (1, 1)]
    return jnp.pad(values, widths)


def to_owners(slots):
    return lax.all_to_all(slots, "tm", split_axis=0, concat_axis=4, tiled=True)


def from_owners(slots):
    return lax.all_to_all(slots, "tm", split_axis=4, concat_axis=0, tiled=True)


def slot_tables(units, filled, step_count):
    index_t = jnp.arange(step_count, dtype=jnp.int32)
    phases = index_t[:, None] * units[None, :] % step_count
    angles = phases.astype(jnp.float32) * (2.0 * math.pi / step_count)
    cosine = jnp.cos(angles)
    sine = jnp.sin(angles)
    parity = (1 - 2 * (index_t % 2)).astype(jnp.float32)
    first = units == 0
    times = index_t.astype(jnp.float32) / step_count
    damping = jnp.exp(times * math.log(ALPHA)) / math.sqrt(step_count)
    growth = jnp.exp(-times * math.log(ALPHA)) / math.sqrt(step_count)
    forward_imag = jnp.where(first[None, :], parity[:, None], -sine)
    forward_table = jnp.stack([cosine, forward_imag], axis=2) * damping[:, None, None]
    weights = jnp.where(first, 1.0, 2.0).astype(jnp.float32)
    inverse_real = cosine * weights[None, :]
    inverse_imag = jnp.where(first[None, :], parity[:, None], -2.0 * sine)
    keep = filled.astype(jnp.float32)[None, :, None]
    inverse_table = jnp.stack([inverse_real, inverse_imag], axis=2) * growth[:, None, None] * keep
    return (forward_table, inverse_table)


def unit_inverse(pair_ids, step_count):
    angles = pair_ids.astype(jnp.float32) * (2.0 * math.pi / step_count)
    ratio = math.exp(math.log(ALPHA) / step_count)
    real_shift = 1.0 + FRICTION - ratio * jnp.cos(angles)
    imag_shift = ratio * jnp.sin(angles)
    denominator = real_shift * real_shift + imag_shift * imag_shift
    real_inv = real_shift / denominator
    imag_inv = -imag_shift / denominator
    is_first = pair_ids == 0
    upper_left = jnp.where(is_first, 1.0 / (1.0 + FRICTION - ratio), real_inv)
    upper_right = jnp.where(is_first, 0.0, -imag_inv)
    lower_left = jnp.where(is_first, 0.0, imag_inv)
    lower_right = jnp.where(is_first, 1.0 / (1.0 + FRICTION + ratio), real_inv)
    return (upper_left, upper_right, lower_left, lower_right)


def apply_inverse(coeffs, values):
    shaped = [c[:, None, None, None] for c in coeffs]
    real_part = values[:, :, 0]
    imag_part = values[:, :, 1]
    new_real = shaped[0] * real_part + shaped[1] * imag_part
    new_imag = shaped[2] * real_part + shaped[3] * imag_part
    return jnp.stack([new_real, new_imag], axis=2)


def flux_fields(state, depth, row_mask):
    height = state[..., 0, :, :] * row_mask
    east = state[..., 1, :, :]
    north = state[..., 2, :, :]
    flux = jnp.stack([height, depth * east, depth * north], axis=-3)
    padded = zero_rim(flux)
    grad_x = padded[..., 0, 1:-1, 2:] - padded[..., 0, 1:-1, :-2]
    grad_y = padded[..., 0, 2:, 1:-1] - padded[..., 0, :-2, 1:-1]
    diverge = (
        padded[..., 1, 1:-1, 2:]
        - padded[..., 1, 1:-1, :-2]
        + (padded[..., 2, 2:, 1:-1] - padded[..., 2, :-2, 1:-1])
    )
    new_height = HALF_COUPLING * diverge
    new_east = HALF_COUPLING * grad_x - CORIOLIS * north
    new_north = HALF_COUPLING * grad_y + CORIOLIS * east
    return jnp.stack([new_height, new_east, new_north], axis=-3)


def apply_parts(coeffs, values):
    shaped = [c[:, None, None, None] for c in coeffs]
    real_part = values[:, 0]
    imag_part = values[:, 1]
    new_real = shaped[0] * real_part + shaped[1] * imag_part
    new_imag = shaped[2] * real_part + shaped[3] * imag_part
    return jnp.stack([new_real, new_imag], axis=1)


def chebyshev(source, start, depth, coeffs, row_mask):
    iterate = start
    for sweep in range(SWEEPS):
        weight = 1.0 / (1.0 + SPREAD * math.cos(math.pi * (2 * sweep + 1) / (2 * SWEEPS)))
        flux = flux_fields(iterate, depth, row_mask)
        update = apply_parts(coeffs, source - flux) - iterate
        iterate = iterate + weight * update
    return iterate


def lat_halo(arrays, width):
    flat = [a.reshape((-1,) + a.shape[-2:]) for a in arrays]
    packed = jnp.concatenate(flat, axis=0)
    rows = packed.shape[1]
    count = lax.axis_size("lat")
    above = lax.ppermute(packed[:, rows - width :], "lat", [(i, i + 1) for i in range(count - 1)])
    below = lax.ppermute(packed[:, :width], "lat", [(i + 1, i) for i in range(count - 1)])
    wide = jnp.concatenate([above, packed, below], axis=1)
    out, offset = [], 0
    for a, f in zip(arrays, flat):
        piece = wide[offset : offset + f.shape[0]]
        out.append(piece.reshape(a.shape[:-2] + piece.shape[1:]))
        offset += f.shape[0]
    return out


def body(trajectory, forcing, initial_state, depth, warm_start, slot_unit, unit_count):
    groups = lax.axis_size("tm")
    position = lax.axis_index("tm")
    local_steps = trajectory.shape[0]
    step_count = local_steps * groups
    rows = depth.shape[0]
    lat_count = lax.axis_size("lat")
    lat_pos = lax.axis_index("lat")
    width = 8 * ((SWEEPS + 7) // 8)

    wide_traj, wide_forcing, wide_initial, wide_depth, wide_start = lat_halo(
        [trajectory, forcing, initial_state, depth, warm_start], width
    )
    flux_term = flux_operator(wide_traj[:, :, None], wide_depth, zero_rim)[:, :, 0]
    partial = wide_forcing - ((1.0 + FRICTION) * wide_traj + flux_term)
    keep = width - SWEEPS + 1
    band = slice(keep, rows + 2 * width - keep)
    moved = lax.all_to_all(
        jnp.stack([wide_traj[:, :, band], partial[:, :, band]], axis=1),
        "tm",
        split_axis=4,
        concat_axis=0,
        tiled=True,
    )
    fields, band_rows, col_count = moved.shape[2], moved.shape[3], moved.shape[4]
    inner = width - keep
    state_cols = jnp.transpose(moved[:, 0, :, inner : inner + rows], (1, 2, 3, 0))
    initial_cols = lax.dynamic_slice_in_dim(
        wide_initial[:, band], position * col_count, col_count, axis=2
    ).reshape(-1)

    flat_units = slot_unit.reshape(-1)
    slot_total = slot_unit.shape[1]
    filled = (jnp.arange(slot_total, dtype=jnp.int32)[None, :] < unit_count[:, None]).reshape(-1)
    forward_table, inverse_table = slot_tables(flat_units, filled, step_count)
    forward = forward_table.reshape(step_count, -1)
    forward_next = jnp.concatenate([forward[1:], jnp.zeros_like(forward[:1])], axis=0)
    stacked = jnp.stack([forward_next, forward], axis=1).reshape(2 * step_count, -1)
    spec = lax.dot_general(
        stacked,
        moved.reshape(2 * step_count, -1),
        (((0,), (0,)), ((), ())),
        precision=lax.Precision.HIGH,
    )
    spec = spec + forward[0][:, None] * initial_cols[None, :]
    outgoing = spec.reshape(groups, slot_total, 2, fields, band_rows, col_count)
    owned = lax.all_to_all(outgoing, "tm", split_axis=0, concat_axis=5, tiled=True)[0]
    pads = ((0, 0), (0, 0), (0, 0), (keep, keep), (0, 0))
    wide_source = jnp.pad(owned, pads)

    own_units = lax.dynamic_index_in_dim(slot_unit, position, 0, keepdims=False)
    own_filled = lax.dynamic_index_in_dim(filled.reshape(groups, -1), position, 0, keepdims=False)
    coeffs = unit_inverse(own_units, step_count)

    global_row = lat_pos * rows - width + jnp.arange(rows + 2 * width, dtype=jnp.int32)
    row_mask = ((global_row >= 0) & (global_row < rows * lat_count)).astype(jnp.float32)
    start = jnp.transpose(wide_start, (0, 2, 1, 3, 4))
    solved = chebyshev(wide_source, start, wide_depth, coeffs, row_mask[:, None])
    solved = solved[:, :, :, width : width + rows]
    spectrum = jnp.where(
        own_filled[:, None, None, None, None], jnp.transpose(solved, (0, 2, 1, 3, 4)), 0.0
    )

    solved_cols = lax.all_to_all(solved[None], "tm", split_axis=5, concat_axis=0, tiled=True)
    corr = lax.dot_general(
        solved_cols.reshape(2 * slot_total * groups, -1),
        inverse_table.reshape(step_count, -1),
        (((0,), (1,)), ((), ())),
        precision=lax.Precision.HIGH,
    )
    updated = state_cols + corr.reshape(state_cols.shape)
    return (updated, spectrum)


def solution(mesh):
    return jax.shard_map(
        body,
        mesh=mesh,
        in_specs=(
            P("tm", None, "lat", None),
            P("tm", None, "lat", None),
            P(None, "lat", None),
            P("lat", None),
            P("tm", None, None, "lat", None),
            P(),
            P(),
        ),
        out_specs=(P(None, "lat", "tm", None), P("tm", None, None, "lat", None)),
        check_vma=False,
    )
```

```python
import math

import jax
import jax.numpy as jnp
from jax import lax
from jax.sharding import PartitionSpec as P

SWEEPS = 6


HALF_COUPLING = 0.125
CORIOLIS = 0.2
FRICTION = 1.0
ALPHA = 0.1
SPREAD = 0.2


def with_halo(cells, sides, width):
    for axis, dim in sides:
        count = lax.axis_size(axis)
        ends = count - 1
        head = lax.slice_in_dim(cells, 0, width, axis=dim)
        tail = lax.slice_in_dim(cells, cells.shape[dim] - width, cells.shape[dim], axis=dim)
        cells = jnp.concatenate(
            [
                lax.ppermute(tail, axis, [(i, (i + 1) % count) for i in range(ends)]),
                cells,
                lax.ppermute(head, axis, [((i + 1) % count, i) for i in range(ends)]),
            ],
            axis=dim,
        )
    return cells


def shifted(value, axis, by):
    size = lax.axis_size(axis)
    pairs = [(i, i + by) for i in range(size) if 0 <= i + by < size]
    return lax.ppermute(value, axis, pairs)


def flux_operator(state, depth, pad_rule, row_mask=None):
    height = state[..., 0:1, :, :, :]
    east = state[..., 1:2, :, :, :]
    north = state[..., 2:3, :, :, :]
    if row_mask is not None:
        height = height * row_mask
    flux = jnp.concatenate([height, depth * east, depth * north], axis=-4)
    padded = pad_rule(flux)
    grad_x = padded[..., 0:1, :, 1:-1, 2:] - padded[..., 0:1, :, 1:-1, :-2]
    grad_y = padded[..., 0:1, :, 2:, 1:-1] - padded[..., 0:1, :, :-2, 1:-1]
    diverge = (
        padded[..., 1:2, :, 1:-1, 2:]
        - padded[..., 1:2, :, 1:-1, :-2]
        + (padded[..., 2:3, :, 2:, 1:-1] - padded[..., 2:3, :, :-2, 1:-1])
    )
    new_height = HALF_COUPLING * diverge
    new_east = HALF_COUPLING * grad_x - CORIOLIS * north
    new_north = HALF_COUPLING * grad_y + CORIOLIS * east
    return jnp.concatenate([new_height, new_east, new_north], axis=-4)


def row_rims(flux):
    rows_done = with_halo(flux, (("lat", 3),), 1)
    return jnp.pad(rows_done, ((0, 0), (0, 0), (0, 0), (0, 0), (1, 1)))


def zero_rim(values):
    widths = [(0, 0)] * (values.ndim - 2) + [(1, 1), (1, 1)]
    return jnp.pad(values, widths)


def to_owners(slots):
    return lax.all_to_all(slots, "tm", split_axis=0, concat_axis=4, tiled=True)


def from_owners(slots):
    return lax.all_to_all(slots, "tm", split_axis=4, concat_axis=0, tiled=True)


def slot_tables(units, filled, step_count):
    index_t = jnp.arange(step_count, dtype=jnp.int32)
    phases = index_t[:, None] * units[None, :] % step_count
    angles = phases.astype(jnp.float32) * (2.0 * math.pi / step_count)
    cosine = jnp.cos(angles)
    sine = jnp.sin(angles)
    parity = (1 - 2 * (index_t % 2)).astype(jnp.float32)
    first = units == 0
    times = index_t.astype(jnp.float32) / step_count
    damping = jnp.exp(times * math.log(ALPHA)) / math.sqrt(step_count)
    growth = jnp.exp(-times * math.log(ALPHA)) / math.sqrt(step_count)
    forward_imag = jnp.where(first[None, :], parity[:, None], -sine)
    forward_table = jnp.stack([cosine, forward_imag], axis=2) * damping[:, None, None]
    weights = jnp.where(first, 1.0, 2.0).astype(jnp.float32)
    inverse_real = cosine * weights[None, :]
    inverse_imag = jnp.where(first[None, :], parity[:, None], -2.0 * sine)
    keep = filled.astype(jnp.float32)[None, :, None]
    inverse_table = jnp.stack([inverse_real, inverse_imag], axis=2) * growth[:, None, None] * keep
    return (forward_table, inverse_table)


def unit_inverse(pair_ids, step_count):
    angles = pair_ids.astype(jnp.float32) * (2.0 * math.pi / step_count)
    ratio = math.exp(math.log(ALPHA) / step_count)
    real_shift = 1.0 + FRICTION - ratio * jnp.cos(angles)
    imag_shift = ratio * jnp.sin(angles)
    denominator = real_shift * real_shift + imag_shift * imag_shift
    real_inv = real_shift / denominator
    imag_inv = -imag_shift / denominator
    is_first = pair_ids == 0
    upper_left = jnp.where(is_first, 1.0 / (1.0 + FRICTION - ratio), real_inv)
    upper_right = jnp.where(is_first, 0.0, -imag_inv)
    lower_left = jnp.where(is_first, 0.0, imag_inv)
    lower_right = jnp.where(is_first, 1.0 / (1.0 + FRICTION + ratio), real_inv)
    return (upper_left, upper_right, lower_left, lower_right)


def apply_inverse(coeffs, values):
    shaped = [c[:, None, None, None] for c in coeffs]
    real_part = values[:, :, 0]
    imag_part = values[:, :, 1]
    new_real = shaped[0] * real_part + shaped[1] * imag_part
    new_imag = shaped[2] * real_part + shaped[3] * imag_part
    return jnp.stack([new_real, new_imag], axis=2)


def chebyshev(source, start, depth, coeffs, row_mask):
    weights = jnp.array(
        [
            1.0 / (1.0 + SPREAD * math.cos(math.pi * (2 * sweep + 1) / (2 * SWEEPS)))
            for sweep in range(SWEEPS)
        ],
        dtype=jnp.float32,
    )

    def sweep_step(sweep, iterate):
        flux = flux_operator(iterate, depth, zero_rim, row_mask)
        update = apply_inverse(coeffs, source - flux) - iterate
        return iterate + weights[sweep] * update

    return lax.fori_loop(0, SWEEPS, sweep_step, start)


def lat_halo(arrays, width):
    flat = [a.reshape((-1,) + a.shape[-2:]) for a in arrays]
    packed = jnp.concatenate(flat, axis=0)
    rows = packed.shape[1]
    count = lax.axis_size("lat")
    above = lax.ppermute(packed[:, rows - width :], "lat", [(i, i + 1) for i in range(count - 1)])
    below = lax.ppermute(packed[:, :width], "lat", [(i + 1, i) for i in range(count - 1)])
    wide = jnp.concatenate([above, packed, below], axis=1)
    out, offset = [], 0
    for a, f in zip(arrays, flat):
        piece = wide[offset : offset + f.shape[0]]
        out.append(piece.reshape(a.shape[:-2] + piece.shape[1:]))
        offset += f.shape[0]
    return out


def body(trajectory, forcing, initial_state, depth, warm_start, slot_unit, unit_count):
    groups = lax.axis_size("tm")
    position = lax.axis_index("tm")
    local_steps = trajectory.shape[0]
    step_count = local_steps * groups
    rows = depth.shape[0]
    lat_count = lax.axis_size("lat")
    lat_pos = lax.axis_index("lat")
    width = 8 * ((SWEEPS + 7) // 8)

    wide_traj, wide_forcing, wide_initial, wide_depth, wide_start = lat_halo(
        [trajectory, forcing, initial_state, depth, warm_start], width
    )
    flux_term = flux_operator(wide_traj[:, :, None], wide_depth, zero_rim)[:, :, 0]
    partial = wide_forcing - ((1.0 + FRICTION) * wide_traj + flux_term)
    keep = width - SWEEPS + 1
    band = slice(keep, rows + 2 * width - keep)
    moved = lax.all_to_all(
        jnp.stack([wide_traj[:, :, band], partial[:, :, band]], axis=1),
        "tm",
        split_axis=4,
        concat_axis=0,
        tiled=True,
    )
    traj_cols, partial_cols = moved[:, 0], moved[:, 1]
    col_count = traj_cols.shape[3]
    initial_cols = lax.dynamic_slice_in_dim(
        wide_initial[:, band], position * col_count, col_count, axis=2
    )
    previous = jnp.concatenate([initial_cols[None], traj_cols[:-1]], axis=0)
    resid_cols = partial_cols + previous
    inner = width - keep
    state_cols = jnp.transpose(traj_cols[:, :, inner : inner + rows], (1, 2, 3, 0))

    flat_units = slot_unit.reshape(-1)
    slot_total = slot_unit.shape[1]
    filled = (jnp.arange(slot_total, dtype=jnp.int32)[None, :] < unit_count[:, None]).reshape(-1)
    forward_table, inverse_table = slot_tables(flat_units, filled, step_count)

    outgoing = jnp.einsum(
        "tsp,tfyx->sfpyx", forward_table, resid_cols, precision=lax.Precision.HIGH
    )
    pads = ((0, 0), (0, 0), (0, 0), (keep, keep), (0, 0))
    wide_source = jnp.pad(to_owners(outgoing), pads)

    own_units = lax.dynamic_index_in_dim(slot_unit, position, 0, keepdims=False)
    own_filled = lax.dynamic_index_in_dim(filled.reshape(groups, -1), position, 0, keepdims=False)
    coeffs = unit_inverse(own_units, step_count)

    global_row = lat_pos * rows - width + jnp.arange(rows + 2 * width, dtype=jnp.int32)
    row_mask = ((global_row >= 0) & (global_row < rows * lat_count)).astype(jnp.float32)
    solved = chebyshev(wide_source, wide_start, wide_depth, coeffs, row_mask[:, None])
    solved = solved[:, :, :, width : width + rows]
    spectrum = jnp.where(own_filled[:, None, None, None, None], solved, 0.0)

    solved_cols = from_owners(solved)
    corr = jnp.einsum(
        "sfpyx,tsp->fyxt", solved_cols, inverse_table, precision=lax.Precision.HIGH
    )
    updated = state_cols + corr
    return (updated, spectrum)


def solution(mesh):
    return jax.shard_map(
        body,
        mesh=mesh,
        in_specs=(
            P("tm", None, "lat", None),
            P("tm", None, "lat", None),
            P(None, "lat", None),
            P("lat", None),
            P("tm", None, None, "lat", None),
            P(),
            P(),
        ),
        out_specs=(P(None, "lat", "tm", None), P("tm", None, None, "lat", None)),
        check_vma=False,
    )
```

```python
import math

import jax
import jax.numpy as jnp
from jax import lax
from jax.sharding import PartitionSpec as P

SWEEPS = 6


HALF_COUPLING = 0.125
CORIOLIS = 0.2
FRICTION = 1.0
ALPHA = 0.1
SPREAD = 0.2


def with_halo(cells, sides, width):
    for axis, dim in sides:
        count = lax.axis_size(axis)
        ends = count - 1
        head = lax.slice_in_dim(cells, 0, width, axis=dim)
        tail = lax.slice_in_dim(cells, cells.shape[dim] - width, cells.shape[dim], axis=dim)
        cells = jnp.concatenate(
            [
                lax.ppermute(tail, axis, [(i, (i + 1) % count) for i in range(ends)]),
                cells,
                lax.ppermute(head, axis, [((i + 1) % count, i) for i in range(ends)]),
            ],
            axis=dim,
        )
    return cells


def shifted(value, axis, by):
    size = lax.axis_size(axis)
    pairs = [(i, i + by) for i in range(size) if 0 <= i + by < size]
    return lax.ppermute(value, axis, pairs)


def flux_operator(state, depth, pad_rule, row_mask=None):
    height = state[..., 0:1, :, :, :]
    east = state[..., 1:2, :, :, :]
    north = state[..., 2:3, :, :, :]
    if row_mask is not None:
        height = height * row_mask
    flux = jnp.concatenate([height, depth * east, depth * north], axis=-4)
    padded = pad_rule(flux)
    grad_x = padded[..., 0:1, :, 1:-1, 2:] - padded[..., 0:1, :, 1:-1, :-2]
    grad_y = padded[..., 0:1, :, 2:, 1:-1] - padded[..., 0:1, :, :-2, 1:-1]
    diverge = (
        padded[..., 1:2, :, 1:-1, 2:]
        - padded[..., 1:2, :, 1:-1, :-2]
        + (padded[..., 2:3, :, 2:, 1:-1] - padded[..., 2:3, :, :-2, 1:-1])
    )
    new_height = HALF_COUPLING * diverge
    new_east = HALF_COUPLING * grad_x - CORIOLIS * north
    new_north = HALF_COUPLING * grad_y + CORIOLIS * east
    return jnp.concatenate([new_height, new_east, new_north], axis=-4)


def row_rims(flux):
    rows_done = with_halo(flux, (("lat", 3),), 1)
    return jnp.pad(rows_done, ((0, 0), (0, 0), (0, 0), (0, 0), (1, 1)))


def zero_rim(values):
    widths = [(0, 0)] * (values.ndim - 2) + [(1, 1), (1, 1)]
    return jnp.pad(values, widths)


def to_owners(slots):
    return lax.all_to_all(slots, "tm", split_axis=0, concat_axis=4, tiled=True)


def from_owners(slots):
    return lax.all_to_all(slots, "tm", split_axis=4, concat_axis=0, tiled=True)


def slot_tables(units, filled, step_count):
    index_t = jnp.arange(step_count, dtype=jnp.int32)
    phases = index_t[:, None] * units[None, :] % step_count
    angles = phases.astype(jnp.float32) * (2.0 * math.pi / step_count)
    cosine = jnp.cos(angles)
    sine = jnp.sin(angles)
    parity = (1 - 2 * (index_t % 2)).astype(jnp.float32)
    first = units == 0
    times = index_t.astype(jnp.float32) / step_count
    damping = jnp.exp(times * math.log(ALPHA)) / math.sqrt(step_count)
    growth = jnp.exp(-times * math.log(ALPHA)) / math.sqrt(step_count)
    forward_imag = jnp.where(first[None, :], parity[:, None], -sine)
    forward_table = jnp.stack([cosine, forward_imag], axis=2) * damping[:, None, None]
    weights = jnp.where(first, 1.0, 2.0).astype(jnp.float32)
    inverse_real = cosine * weights[None, :]
    inverse_imag = jnp.where(first[None, :], parity[:, None], -2.0 * sine)
    keep = filled.astype(jnp.float32)[None, :, None]
    inverse_table = jnp.stack([inverse_real, inverse_imag], axis=2) * growth[:, None, None] * keep
    return (forward_table, inverse_table)


def unit_inverse(pair_ids, step_count):
    angles = pair_ids.astype(jnp.float32) * (2.0 * math.pi / step_count)
    ratio = math.exp(math.log(ALPHA) / step_count)
    real_shift = 1.0 + FRICTION - ratio * jnp.cos(angles)
    imag_shift = ratio * jnp.sin(angles)
    denominator = real_shift * real_shift + imag_shift * imag_shift
    real_inv = real_shift / denominator
    imag_inv = -imag_shift / denominator
    is_first = pair_ids == 0
    upper_left = jnp.where(is_first, 1.0 / (1.0 + FRICTION - ratio), real_inv)
    upper_right = jnp.where(is_first, 0.0, -imag_inv)
    lower_left = jnp.where(is_first, 0.0, imag_inv)
    lower_right = jnp.where(is_first, 1.0 / (1.0 + FRICTION + ratio), real_inv)
    return (upper_left, upper_right, lower_left, lower_right)


def apply_inverse(coeffs, values):
    shaped = [c[:, None, None, None] for c in coeffs]
    real_part = values[:, :, 0]
    imag_part = values[:, :, 1]
    new_real = shaped[0] * real_part + shaped[1] * imag_part
    new_imag = shaped[2] * real_part + shaped[3] * imag_part
    return jnp.stack([new_real, new_imag], axis=2)


def chebyshev(source, start, depth, coeffs, row_mask):
    iterate = start
    for sweep in range(SWEEPS):
        weight = 1.0 / (1.0 + SPREAD * math.cos(math.pi * (2 * sweep + 1) / (2 * SWEEPS)))
        flux = flux_operator(iterate, depth, zero_rim, row_mask)
        update = apply_inverse(coeffs, source - flux) - iterate
        iterate = iterate + weight * update
    return iterate


def lat_halo(arrays, width, sent):
    flat = [a.reshape((-1,) + a.shape[-2:]) for a in arrays]
    packed = jnp.concatenate(flat, axis=0)
    rows = packed.shape[1]
    count = lax.axis_size("lat")
    above = lax.ppermute(packed[:, rows - sent :], "lat", [(i, i + 1) for i in range(count - 1)])
    below = lax.ppermute(packed[:, :sent], "lat", [(i + 1, i) for i in range(count - 1)])
    blank = jnp.zeros((packed.shape[0], width - sent, packed.shape[2]), packed.dtype)
    wide = jnp.concatenate([blank, above, packed, below, blank], axis=1)
    out, offset = [], 0
    for a, f in zip(arrays, flat):
        piece = wide[offset : offset + f.shape[0]]
        out.append(piece.reshape(a.shape[:-2] + piece.shape[1:]))
        offset += f.shape[0]
    return out


def body(trajectory, forcing, initial_state, depth, warm_start, slot_unit, unit_count):
    groups = lax.axis_size("tm")
    position = lax.axis_index("tm")
    local_steps = trajectory.shape[0]
    step_count = local_steps * groups
    rows = depth.shape[0]
    lat_count = lax.axis_size("lat")
    lat_pos = lax.axis_index("lat")
    width = 8 * ((SWEEPS + 7) // 8)

    wide_traj, wide_forcing, wide_initial, wide_depth = lat_halo(
        [trajectory, forcing, initial_state, depth], width, SWEEPS
    )
    (wide_start,) = lat_halo([warm_start], width, SWEEPS)
    flux_term = flux_operator(wide_traj[:, :, None], wide_depth, zero_rim)[:, :, 0]
    partial = wide_forcing - ((1.0 + FRICTION) * wide_traj + flux_term)
    keep = width - SWEEPS + 1
    band = slice(keep, rows + 2 * width - keep)
    moved = lax.all_to_all(
        jnp.stack([wide_traj[:, :, band], partial[:, :, band]], axis=1),
        "tm",
        split_axis=4,
        concat_axis=0,
        tiled=True,
    )
    traj_cols, partial_cols = moved[:, 0], moved[:, 1]
    col_count = traj_cols.shape[3]
    initial_cols = lax.dynamic_slice_in_dim(
        wide_initial[:, band], position * col_count, col_count, axis=2
    )
    previous = jnp.concatenate([initial_cols[None], traj_cols[:-1]], axis=0)
    resid_cols = partial_cols + previous
    inner = width - keep
    state_cols = jnp.transpose(traj_cols[:, :, inner : inner + rows], (1, 2, 3, 0))

    flat_units = slot_unit.reshape(-1)
    slot_total = slot_unit.shape[1]
    filled = (jnp.arange(slot_total, dtype=jnp.int32)[None, :] < unit_count[:, None]).reshape(-1)
    forward_table, inverse_table = slot_tables(flat_units, filled, step_count)

    outgoing = jnp.einsum(
        "tsp,tfyx->sfpyx", forward_table, resid_cols, precision=lax.Precision.HIGH
    )
    pads = ((0, 0), (0, 0), (0, 0), (keep, keep), (0, 0))
    wide_source = jnp.pad(to_owners(outgoing), pads)

    own_units = lax.dynamic_index_in_dim(slot_unit, position, 0, keepdims=False)
    own_filled = lax.dynamic_index_in_dim(filled.reshape(groups, -1), position, 0, keepdims=False)
    coeffs = unit_inverse(own_units, step_count)

    global_row = lat_pos * rows - width + jnp.arange(rows + 2 * width, dtype=jnp.int32)
    row_mask = ((global_row >= 0) & (global_row < rows * lat_count)).astype(jnp.float32)
    solved = chebyshev(wide_source, wide_start, wide_depth, coeffs, row_mask[:, None])
    solved = solved[:, :, :, width : width + rows]
    spectrum = jnp.where(own_filled[:, None, None, None, None], solved, 0.0)

    solved_cols = from_owners(solved)
    corr = jnp.einsum(
        "sfpyx,tsp->fyxt", solved_cols, inverse_table, precision=lax.Precision.HIGH
    )
    updated = state_cols + corr
    return (updated, spectrum)


def solution(mesh):
    return jax.shard_map(
        body,
        mesh=mesh,
        in_specs=(
            P("tm", None, "lat", None),
            P("tm", None, "lat", None),
            P(None, "lat", None),
            P("lat", None),
            P("tm", None, None, "lat", None),
            P(),
            P(),
        ),
        out_specs=(P(None, "lat", "tm", None), P("tm", None, None, "lat", None)),
        check_vma=False,
    )
```

```python
import math

import jax
import jax.numpy as jnp
from jax import lax
from jax.sharding import PartitionSpec as P

SWEEPS = 6


HALF_COUPLING = 0.125
CORIOLIS = 0.2
FRICTION = 1.0
ALPHA = 0.1
SPREAD = 0.2


def with_halo(cells, sides, width):
    for axis, dim in sides:
        count = lax.axis_size(axis)
        ends = count - 1
        head = lax.slice_in_dim(cells, 0, width, axis=dim)
        tail = lax.slice_in_dim(cells, cells.shape[dim] - width, cells.shape[dim], axis=dim)
        cells = jnp.concatenate(
            [
                lax.ppermute(tail, axis, [(i, (i + 1) % count) for i in range(ends)]),
                cells,
                lax.ppermute(head, axis, [((i + 1) % count, i) for i in range(ends)]),
            ],
            axis=dim,
        )
    return cells


def shifted(value, axis, by):
    size = lax.axis_size(axis)
    pairs = [(i, i + by) for i in range(size) if 0 <= i + by < size]
    return lax.ppermute(value, axis, pairs)


def flux_operator(state, depth, pad_rule, row_mask=None):
    height = state[..., 0:1, :, :, :]
    east = state[..., 1:2, :, :, :]
    north = state[..., 2:3, :, :, :]
    if row_mask is not None:
        height = height * row_mask
    flux = jnp.concatenate([height, depth * east, depth * north], axis=-4)
    padded = pad_rule(flux)
    grad_x = padded[..., 0:1, :, 1:-1, 2:] - padded[..., 0:1, :, 1:-1, :-2]
    grad_y = padded[..., 0:1, :, 2:, 1:-1] - padded[..., 0:1, :, :-2, 1:-1]
    diverge = (
        padded[..., 1:2, :, 1:-1, 2:]
        - padded[..., 1:2, :, 1:-1, :-2]
        + (padded[..., 2:3, :, 2:, 1:-1] - padded[..., 2:3, :, :-2, 1:-1])
    )
    new_height = HALF_COUPLING * diverge
    new_east = HALF_COUPLING * grad_x - CORIOLIS * north
    new_north = HALF_COUPLING * grad_y + CORIOLIS * east
    return jnp.concatenate([new_height, new_east, new_north], axis=-4)


def row_rims(flux):
    rows_done = with_halo(flux, (("lat", 3),), 1)
    return jnp.pad(rows_done, ((0, 0), (0, 0), (0, 0), (0, 0), (1, 1)))


def zero_rim(values):
    widths = [(0, 0)] * (values.ndim - 2) + [(1, 1), (1, 1)]
    return jnp.pad(values, widths)


def to_owners(slots):
    return lax.all_to_all(slots, "tm", split_axis=0, concat_axis=4, tiled=True)


def from_owners(slots):
    return lax.all_to_all(slots, "tm", split_axis=4, concat_axis=0, tiled=True)


def slot_tables(units, filled, step_count):
    index_t = jnp.arange(step_count, dtype=jnp.int32)
    phases = index_t[:, None] * units[None, :] % step_count
    angles = phases.astype(jnp.float32) * (2.0 * math.pi / step_count)
    cosine = jnp.cos(angles)
    sine = jnp.sin(angles)
    parity = (1 - 2 * (index_t % 2)).astype(jnp.float32)
    first = units == 0
    times = index_t.astype(jnp.float32) / step_count
    damping = jnp.exp(times * math.log(ALPHA)) / math.sqrt(step_count)
    growth = jnp.exp(-times * math.log(ALPHA)) / math.sqrt(step_count)
    forward_imag = jnp.where(first[None, :], parity[:, None], -sine)
    forward_table = jnp.stack([cosine, forward_imag], axis=2) * damping[:, None, None]
    weights = jnp.where(first, 1.0, 2.0).astype(jnp.float32)
    inverse_real = cosine * weights[None, :]
    inverse_imag = jnp.where(first[None, :], parity[:, None], -2.0 * sine)
    keep = filled.astype(jnp.float32)[None, :, None]
    inverse_table = jnp.stack([inverse_real, inverse_imag], axis=2) * growth[:, None, None] * keep
    return (forward_table, inverse_table)


def unit_inverse(pair_ids, step_count):
    angles = pair_ids.astype(jnp.float32) * (2.0 * math.pi / step_count)
    ratio = math.exp(math.log(ALPHA) / step_count)
    real_shift = 1.0 + FRICTION - ratio * jnp.cos(angles)
    imag_shift = ratio * jnp.sin(angles)
    denominator = real_shift * real_shift + imag_shift * imag_shift
    real_inv = real_shift / denominator
    imag_inv = -imag_shift / denominator
    is_first = pair_ids == 0
    upper_left = jnp.where(is_first, 1.0 / (1.0 + FRICTION - ratio), real_inv)
    upper_right = jnp.where(is_first, 0.0, -imag_inv)
    lower_left = jnp.where(is_first, 0.0, imag_inv)
    lower_right = jnp.where(is_first, 1.0 / (1.0 + FRICTION + ratio), real_inv)
    return (upper_left, upper_right, lower_left, lower_right)


def apply_inverse(coeffs, values):
    shaped = [c[:, None, None, None] for c in coeffs]
    real_part = values[:, :, 0]
    imag_part = values[:, :, 1]
    new_real = shaped[0] * real_part + shaped[1] * imag_part
    new_imag = shaped[2] * real_part + shaped[3] * imag_part
    return jnp.stack([new_real, new_imag], axis=2)


def chebyshev(source, start, depth, coeffs, row_mask):
    iterate = start
    for sweep in range(SWEEPS):
        weight = 1.0 / (1.0 + SPREAD * math.cos(math.pi * (2 * sweep + 1) / (2 * SWEEPS)))
        flux = flux_operator(iterate, depth, zero_rim, row_mask)
        update = apply_inverse(coeffs, source - flux) - iterate
        iterate = iterate + weight * update
    return iterate


def lat_halo(arrays, width, sent):
    flat = [a.reshape((-1,) + a.shape[-2:]) for a in arrays]
    packed = jnp.concatenate(flat, axis=0)
    rows = packed.shape[1]
    count = lax.axis_size("lat")
    above = lax.ppermute(packed[:, rows - sent :], "lat", [(i, i + 1) for i in range(count - 1)])
    below = lax.ppermute(packed[:, :sent], "lat", [(i + 1, i) for i in range(count - 1)])
    blank = jnp.zeros((packed.shape[0], width - sent, packed.shape[2]), packed.dtype)
    wide = jnp.concatenate([blank, above, packed, below, blank], axis=1)
    out, offset = [], 0
    for a, f in zip(arrays, flat):
        piece = wide[offset : offset + f.shape[0]]
        out.append(piece.reshape(a.shape[:-2] + piece.shape[1:]))
        offset += f.shape[0]
    return out


def body(trajectory, forcing, initial_state, depth, warm_start, slot_unit, unit_count):
    groups = lax.axis_size("tm")
    position = lax.axis_index("tm")
    local_steps = trajectory.shape[0]
    step_count = local_steps * groups
    rows = depth.shape[0]
    lat_count = lax.axis_size("lat")
    lat_pos = lax.axis_index("lat")
    width = 8 * ((SWEEPS + 7) // 8)

    wide_traj, wide_forcing, wide_initial, wide_depth = lat_halo(
        [trajectory, forcing, initial_state, depth], width, SWEEPS
    )
    flux_term = flux_operator(wide_traj[:, :, None], wide_depth, zero_rim)[:, :, 0]
    partial = wide_forcing - ((1.0 + FRICTION) * wide_traj + flux_term)
    keep = width - SWEEPS + 1
    band = slice(keep, rows + 2 * width - keep)
    outgoing_rows, warm_start = lax.optimization_barrier(
        (jnp.stack([wide_traj[:, :, band], partial[:, :, band]], axis=1), warm_start)
    )
    (wide_start,) = lat_halo([warm_start], width, SWEEPS)
    moved = lax.all_to_all(
        outgoing_rows,
        "tm",
        split_axis=4,
        concat_axis=0,
        tiled=True,
    )
    traj_cols, partial_cols = moved[:, 0], moved[:, 1]
    col_count = traj_cols.shape[3]
    initial_cols = lax.dynamic_slice_in_dim(
        wide_initial[:, band], position * col_count, col_count, axis=2
    )
    previous = jnp.concatenate([initial_cols[None], traj_cols[:-1]], axis=0)
    resid_cols = partial_cols + previous
    inner = width - keep
    state_cols = jnp.transpose(traj_cols[:, :, inner : inner + rows], (1, 2, 3, 0))

    flat_units = slot_unit.reshape(-1)
    slot_total = slot_unit.shape[1]
    filled = (jnp.arange(slot_total, dtype=jnp.int32)[None, :] < unit_count[:, None]).reshape(-1)
    forward_table, inverse_table = slot_tables(flat_units, filled, step_count)

    outgoing = jnp.einsum(
        "tsp,tfyx->sfpyx", forward_table, resid_cols, precision=lax.Precision.HIGH
    )
    pads = ((0, 0), (0, 0), (0, 0), (keep, keep), (0, 0))
    wide_source = jnp.pad(to_owners(outgoing), pads)

    own_units = lax.dynamic_index_in_dim(slot_unit, position, 0, keepdims=False)
    own_filled = lax.dynamic_index_in_dim(filled.reshape(groups, -1), position, 0, keepdims=False)
    coeffs = unit_inverse(own_units, step_count)

    global_row = lat_pos * rows - width + jnp.arange(rows + 2 * width, dtype=jnp.int32)
    row_mask = ((global_row >= 0) & (global_row < rows * lat_count)).astype(jnp.float32)
    solved = chebyshev(wide_source, wide_start, wide_depth, coeffs, row_mask[:, None])
    solved = solved[:, :, :, width : width + rows]
    spectrum = jnp.where(own_filled[:, None, None, None, None], solved, 0.0)

    solved_cols = from_owners(solved)
    corr = jnp.einsum(
        "sfpyx,tsp->fyxt", solved_cols, inverse_table, precision=lax.Precision.HIGH
    )
    updated = state_cols + corr
    return (updated, spectrum)


def solution(mesh):
    return jax.shard_map(
        body,
        mesh=mesh,
        in_specs=(
            P("tm", None, "lat", None),
            P("tm", None, "lat", None),
            P(None, "lat", None),
            P("lat", None),
            P("tm", None, None, "lat", None),
            P(),
            P(),
        ),
        out_specs=(P(None, "lat", "tm", None), P("tm", None, None, "lat", None)),
        check_vma=False,
    )
```

```python
import math

import jax
import jax.numpy as jnp
from jax import lax
from jax.sharding import PartitionSpec as P

SWEEPS = 6


HALF_COUPLING = 0.125
CORIOLIS = 0.2
FRICTION = 1.0
ALPHA = 0.1
SPREAD = 0.2


def with_halo(cells, sides, width):
    for axis, dim in sides:
        count = lax.axis_size(axis)
        ends = count - 1
        head = lax.slice_in_dim(cells, 0, width, axis=dim)
        tail = lax.slice_in_dim(cells, cells.shape[dim] - width, cells.shape[dim], axis=dim)
        cells = jnp.concatenate(
            [
                lax.ppermute(tail, axis, [(i, (i + 1) % count) for i in range(ends)]),
                cells,
                lax.ppermute(head, axis, [((i + 1) % count, i) for i in range(ends)]),
            ],
            axis=dim,
        )
    return cells


def shifted(value, axis, by):
    size = lax.axis_size(axis)
    pairs = [(i, i + by) for i in range(size) if 0 <= i + by < size]
    return lax.ppermute(value, axis, pairs)


def flux_operator(state, depth, pad_rule, row_mask=None):
    height = state[..., 0:1, :, :, :]
    east = state[..., 1:2, :, :, :]
    north = state[..., 2:3, :, :, :]
    if row_mask is not None:
        height = height * row_mask
    flux = jnp.concatenate([height, depth * east, depth * north], axis=-4)
    padded = pad_rule(flux)
    grad_x = padded[..., 0:1, :, 1:-1, 2:] - padded[..., 0:1, :, 1:-1, :-2]
    grad_y = padded[..., 0:1, :, 2:, 1:-1] - padded[..., 0:1, :, :-2, 1:-1]
    diverge = (
        padded[..., 1:2, :, 1:-1, 2:]
        - padded[..., 1:2, :, 1:-1, :-2]
        + (padded[..., 2:3, :, 2:, 1:-1] - padded[..., 2:3, :, :-2, 1:-1])
    )
    new_height = HALF_COUPLING * diverge
    new_east = HALF_COUPLING * grad_x - CORIOLIS * north
    new_north = HALF_COUPLING * grad_y + CORIOLIS * east
    return jnp.concatenate([new_height, new_east, new_north], axis=-4)


def row_rims(flux):
    rows_done = with_halo(flux, (("lat", 3),), 1)
    return jnp.pad(rows_done, ((0, 0), (0, 0), (0, 0), (0, 0), (1, 1)))


def zero_rim(values):
    widths = [(0, 0)] * (values.ndim - 2) + [(1, 1), (1, 1)]
    return jnp.pad(values, widths)


def to_owners(slots):
    return lax.all_to_all(slots, "tm", split_axis=0, concat_axis=4, tiled=True)


def from_owners(slots):
    return lax.all_to_all(slots, "tm", split_axis=4, concat_axis=0, tiled=True)


def slot_tables(units, filled, step_count):
    index_t = jnp.arange(step_count, dtype=jnp.int32)
    phases = index_t[:, None] * units[None, :] % step_count
    angles = phases.astype(jnp.float32) * (2.0 * math.pi / step_count)
    cosine = jnp.cos(angles)
    sine = jnp.sin(angles)
    parity = (1 - 2 * (index_t % 2)).astype(jnp.float32)
    first = units == 0
    times = index_t.astype(jnp.float32) / step_count
    damping = jnp.exp(times * math.log(ALPHA)) / math.sqrt(step_count)
    growth = jnp.exp(-times * math.log(ALPHA)) / math.sqrt(step_count)
    forward_imag = jnp.where(first[None, :], parity[:, None], -sine)
    forward_table = jnp.stack([cosine, forward_imag], axis=2) * damping[:, None, None]
    weights = jnp.where(first, 1.0, 2.0).astype(jnp.float32)
    inverse_real = cosine * weights[None, :]
    inverse_imag = jnp.where(first[None, :], parity[:, None], -2.0 * sine)
    keep = filled.astype(jnp.float32)[None, :, None]
    inverse_table = jnp.stack([inverse_real, inverse_imag], axis=2) * growth[:, None, None] * keep
    return (forward_table, inverse_table)


def unit_inverse(pair_ids, step_count):
    angles = pair_ids.astype(jnp.float32) * (2.0 * math.pi / step_count)
    ratio = math.exp(math.log(ALPHA) / step_count)
    real_shift = 1.0 + FRICTION - ratio * jnp.cos(angles)
    imag_shift = ratio * jnp.sin(angles)
    denominator = real_shift * real_shift + imag_shift * imag_shift
    real_inv = real_shift / denominator
    imag_inv = -imag_shift / denominator
    is_first = pair_ids == 0
    upper_left = jnp.where(is_first, 1.0 / (1.0 + FRICTION - ratio), real_inv)
    upper_right = jnp.where(is_first, 0.0, -imag_inv)
    lower_left = jnp.where(is_first, 0.0, imag_inv)
    lower_right = jnp.where(is_first, 1.0 / (1.0 + FRICTION + ratio), real_inv)
    return (upper_left, upper_right, lower_left, lower_right)


def apply_inverse(coeffs, values):
    shaped = [c[:, None, None, None] for c in coeffs]
    real_part = values[:, :, 0]
    imag_part = values[:, :, 1]
    new_real = shaped[0] * real_part + shaped[1] * imag_part
    new_imag = shaped[2] * real_part + shaped[3] * imag_part
    return jnp.stack([new_real, new_imag], axis=2)


def chebyshev(source, start, depth, coeffs, row_mask):
    iterate = start
    for sweep in range(SWEEPS):
        weight = 1.0 / (1.0 + SPREAD * math.cos(math.pi * (2 * sweep + 1) / (2 * SWEEPS)))
        flux = flux_operator(iterate, depth, zero_rim, row_mask)
        update = apply_inverse(coeffs, source - flux) - iterate
        iterate = iterate + weight * update
    return iterate


def lat_halo(arrays, width, sent):
    flat = [a.reshape((-1,) + a.shape[-2:]) for a in arrays]
    packed = jnp.concatenate(flat, axis=0)
    rows = packed.shape[1]
    count = lax.axis_size("lat")
    above = lax.ppermute(packed[:, rows - sent :], "lat", [(i, i + 1) for i in range(count - 1)])
    below = lax.ppermute(packed[:, :sent], "lat", [(i + 1, i) for i in range(count - 1)])
    blank = jnp.zeros((packed.shape[0], width - sent, packed.shape[2]), packed.dtype)
    wide = jnp.concatenate([blank, above, packed, below, blank], axis=1)
    out, offset = [], 0
    for a, f in zip(arrays, flat):
        piece = wide[offset : offset + f.shape[0]]
        out.append(piece.reshape(a.shape[:-2] + piece.shape[1:]))
        offset += f.shape[0]
    return out


def body(trajectory, forcing, initial_state, depth, warm_start, slot_unit, unit_count):
    groups = lax.axis_size("tm")
    position = lax.axis_index("tm")
    local_steps = trajectory.shape[0]
    step_count = local_steps * groups
    rows = depth.shape[0]
    lat_count = lax.axis_size("lat")
    lat_pos = lax.axis_index("lat")
    width = 8 * ((SWEEPS + 7) // 8)

    wide_traj, wide_forcing, wide_initial, wide_depth = lat_halo(
        [trajectory, forcing, initial_state, depth], width, SWEEPS
    )
    flux_term = flux_operator(wide_traj[:, :, None], wide_depth, zero_rim)[:, :, 0]
    partial = wide_forcing - ((1.0 + FRICTION) * wide_traj + flux_term)
    keep = width - SWEEPS + 1
    band = slice(keep, rows + 2 * width - keep)
    outgoing_rows, warm_start = lax.optimization_barrier(
        (jnp.stack([wide_traj[:, :, band], partial[:, :, band]], axis=1), warm_start)
    )
    (wide_start,) = lat_halo([warm_start], width, SWEEPS)
    moved = lax.all_to_all(
        outgoing_rows,
        "tm",
        split_axis=4,
        concat_axis=0,
        tiled=True,
    )
    moved, wide_start = lax.optimization_barrier((moved, wide_start))
    traj_cols, partial_cols = moved[:, 0], moved[:, 1]
    col_count = traj_cols.shape[3]
    initial_cols = lax.dynamic_slice_in_dim(
        wide_initial[:, band], position * col_count, col_count, axis=2
    )
    previous = jnp.concatenate([initial_cols[None], traj_cols[:-1]], axis=0)
    resid_cols = partial_cols + previous
    inner = width - keep
    state_cols = jnp.transpose(traj_cols[:, :, inner : inner + rows], (1, 2, 3, 0))

    flat_units = slot_unit.reshape(-1)
    slot_total = slot_unit.shape[1]
    filled = (jnp.arange(slot_total, dtype=jnp.int32)[None, :] < unit_count[:, None]).reshape(-1)
    forward_table, inverse_table = slot_tables(flat_units, filled, step_count)

    outgoing = jnp.einsum(
        "tsp,tfyx->sfpyx", forward_table, resid_cols, precision=lax.Precision.HIGH
    )
    pads = ((0, 0), (0, 0), (0, 0), (keep, keep), (0, 0))
    wide_source = jnp.pad(to_owners(outgoing), pads)

    own_units = lax.dynamic_index_in_dim(slot_unit, position, 0, keepdims=False)
    own_filled = lax.dynamic_index_in_dim(filled.reshape(groups, -1), position, 0, keepdims=False)
    coeffs = unit_inverse(own_units, step_count)

    global_row = lat_pos * rows - width + jnp.arange(rows + 2 * width, dtype=jnp.int32)
    row_mask = ((global_row >= 0) & (global_row < rows * lat_count)).astype(jnp.float32)
    solved = chebyshev(wide_source, wide_start, wide_depth, coeffs, row_mask[:, None])
    solved = solved[:, :, :, width : width + rows]
    spectrum = jnp.where(own_filled[:, None, None, None, None], solved, 0.0)

    solved_cols = from_owners(solved)
    corr = jnp.einsum(
        "sfpyx,tsp->fyxt", solved_cols, inverse_table, precision=lax.Precision.HIGH
    )
    updated = state_cols + corr
    return (updated, spectrum)


def solution(mesh):
    return jax.shard_map(
        body,
        mesh=mesh,
        in_specs=(
            P("tm", None, "lat", None),
            P("tm", None, "lat", None),
            P(None, "lat", None),
            P("lat", None),
            P("tm", None, None, "lat", None),
            P(),
            P(),
        ),
        out_specs=(P(None, "lat", "tm", None), P("tm", None, None, "lat", None)),
        check_vma=False,
    )
```

```python
import math

import jax
import jax.numpy as jnp
from jax import lax
from jax.sharding import PartitionSpec as P

SWEEPS = 6


HALF_COUPLING = 0.125
CORIOLIS = 0.2
FRICTION = 1.0
ALPHA = 0.1
SPREAD = 0.2


def with_halo(cells, sides, width):
    for axis, dim in sides:
        count = lax.axis_size(axis)
        ends = count - 1
        head = lax.slice_in_dim(cells, 0, width, axis=dim)
        tail = lax.slice_in_dim(cells, cells.shape[dim] - width, cells.shape[dim], axis=dim)
        cells = jnp.concatenate(
            [
                lax.ppermute(tail, axis, [(i, (i + 1) % count) for i in range(ends)]),
                cells,
                lax.ppermute(head, axis, [((i + 1) % count, i) for i in range(ends)]),
            ],
            axis=dim,
        )
    return cells


def shifted(value, axis, by):
    size = lax.axis_size(axis)
    pairs = [(i, i + by) for i in range(size) if 0 <= i + by < size]
    return lax.ppermute(value, axis, pairs)


def flux_operator(state, depth, pad_rule, row_mask=None):
    height = state[..., 0:1, :, :, :]
    east = state[..., 1:2, :, :, :]
    north = state[..., 2:3, :, :, :]
    if row_mask is not None:
        height = height * row_mask
    flux = jnp.concatenate([height, depth * east, depth * north], axis=-4)
    padded = pad_rule(flux)
    grad_x = padded[..., 0:1, :, 1:-1, 2:] - padded[..., 0:1, :, 1:-1, :-2]
    grad_y = padded[..., 0:1, :, 2:, 1:-1] - padded[..., 0:1, :, :-2, 1:-1]
    diverge = (
        padded[..., 1:2, :, 1:-1, 2:]
        - padded[..., 1:2, :, 1:-1, :-2]
        + (padded[..., 2:3, :, 2:, 1:-1] - padded[..., 2:3, :, :-2, 1:-1])
    )
    new_height = HALF_COUPLING * diverge
    new_east = HALF_COUPLING * grad_x - CORIOLIS * north
    new_north = HALF_COUPLING * grad_y + CORIOLIS * east
    return jnp.concatenate([new_height, new_east, new_north], axis=-4)


def row_rims(flux):
    rows_done = with_halo(flux, (("lat", 3),), 1)
    return jnp.pad(rows_done, ((0, 0), (0, 0), (0, 0), (0, 0), (1, 1)))


def zero_rim(values):
    widths = [(0, 0)] * (values.ndim - 2) + [(1, 1), (1, 1)]
    return jnp.pad(values, widths)


def to_owners(slots):
    return lax.all_to_all(slots, "tm", split_axis=0, concat_axis=4, tiled=True)


def from_owners(slots):
    return lax.all_to_all(slots, "tm", split_axis=4, concat_axis=0, tiled=True)


def slot_tables(units, filled, step_count):
    index_t = jnp.arange(step_count, dtype=jnp.int32)
    phases = index_t[:, None] * units[None, :] % step_count
    angles = phases.astype(jnp.float32) * (2.0 * math.pi / step_count)
    cosine = jnp.cos(angles)
    sine = jnp.sin(angles)
    parity = (1 - 2 * (index_t % 2)).astype(jnp.float32)
    first = units == 0
    times = index_t.astype(jnp.float32) / step_count
    damping = jnp.exp(times * math.log(ALPHA)) / math.sqrt(step_count)
    growth = jnp.exp(-times * math.log(ALPHA)) / math.sqrt(step_count)
    forward_imag = jnp.where(first[None, :], parity[:, None], -sine)
    forward_table = jnp.stack([cosine, forward_imag], axis=2) * damping[:, None, None]
    weights = jnp.where(first, 1.0, 2.0).astype(jnp.float32)
    inverse_real = cosine * weights[None, :]
    inverse_imag = jnp.where(first[None, :], parity[:, None], -2.0 * sine)
    keep = filled.astype(jnp.float32)[None, :, None]
    inverse_table = jnp.stack([inverse_real, inverse_imag], axis=2) * growth[:, None, None] * keep
    return (forward_table, inverse_table)


def unit_inverse(pair_ids, step_count):
    angles = pair_ids.astype(jnp.float32) * (2.0 * math.pi / step_count)
    ratio = math.exp(math.log(ALPHA) / step_count)
    real_shift = 1.0 + FRICTION - ratio * jnp.cos(angles)
    imag_shift = ratio * jnp.sin(angles)
    denominator = real_shift * real_shift + imag_shift * imag_shift
    real_inv = real_shift / denominator
    imag_inv = -imag_shift / denominator
    is_first = pair_ids == 0
    upper_left = jnp.where(is_first, 1.0 / (1.0 + FRICTION - ratio), real_inv)
    upper_right = jnp.where(is_first, 0.0, -imag_inv)
    lower_left = jnp.where(is_first, 0.0, imag_inv)
    lower_right = jnp.where(is_first, 1.0 / (1.0 + FRICTION + ratio), real_inv)
    return (upper_left, upper_right, lower_left, lower_right)


def apply_inverse(coeffs, values):
    shaped = [c[:, None, None, None] for c in coeffs]
    real_part = values[:, :, 0]
    imag_part = values[:, :, 1]
    new_real = shaped[0] * real_part + shaped[1] * imag_part
    new_imag = shaped[2] * real_part + shaped[3] * imag_part
    return jnp.stack([new_real, new_imag], axis=2)


def chebyshev(source, start, depth, coeffs, row_mask):
    iterate = start
    for sweep in range(SWEEPS):
        weight = 1.0 / (1.0 + SPREAD * math.cos(math.pi * (2 * sweep + 1) / (2 * SWEEPS)))
        flux = flux_operator(iterate, depth, zero_rim, row_mask)
        update = apply_inverse(coeffs, source - flux) - iterate
        iterate = iterate + weight * update
    return iterate


def lat_halo(arrays, width, sent):
    flat = [a.reshape((-1,) + a.shape[-2:]) for a in arrays]
    packed = jnp.concatenate(flat, axis=0)
    rows = packed.shape[1]
    count = lax.axis_size("lat")
    above = lax.ppermute(packed[:, rows - sent :], "lat", [(i, i + 1) for i in range(count - 1)])
    below = lax.ppermute(packed[:, :sent], "lat", [(i + 1, i) for i in range(count - 1)])
    blank = jnp.zeros((packed.shape[0], width - sent, packed.shape[2]), packed.dtype)
    wide = jnp.concatenate([blank, above, packed, below, blank], axis=1)
    out, offset = [], 0
    for a, f in zip(arrays, flat):
        piece = wide[offset : offset + f.shape[0]]
        out.append(piece.reshape(a.shape[:-2] + piece.shape[1:]))
        offset += f.shape[0]
    return out


def body(trajectory, forcing, initial_state, depth, warm_start, slot_unit, unit_count):
    groups = lax.axis_size("tm")
    position = lax.axis_index("tm")
    local_steps = trajectory.shape[0]
    step_count = local_steps * groups
    rows = depth.shape[0]
    lat_count = lax.axis_size("lat")
    lat_pos = lax.axis_index("lat")
    width = 8 * ((SWEEPS + 7) // 8)

    wide_traj, wide_forcing, wide_initial, wide_depth = lat_halo(
        [trajectory, forcing, initial_state, depth], width, SWEEPS
    )
    flux_term = flux_operator(wide_traj[:, :, None], wide_depth, zero_rim)[:, :, 0]
    partial = wide_forcing - ((1.0 + FRICTION) * wide_traj + flux_term)
    keep = width - SWEEPS + 1
    band = slice(keep, rows + 2 * width - keep)
    outgoing_rows, warm_start = lax.optimization_barrier(
        (jnp.stack([wide_traj[:, :, band], partial[:, :, band]], axis=1), warm_start)
    )
    (wide_start,) = lat_halo([warm_start], width, SWEEPS)
    lead = outgoing_rows.shape[:-1]
    split_rows = outgoing_rows.reshape(lead + (groups, -1))
    split_rows = jnp.moveaxis(split_rows, -2, 0)
    moved = lax.all_to_all(split_rows, "tm", 0, 0, tiled=False)
    moved = moved.reshape((-1,) + moved.shape[2:])
    traj_cols, partial_cols = moved[:, 0], moved[:, 1]
    col_count = traj_cols.shape[3]
    initial_cols = lax.dynamic_slice_in_dim(
        wide_initial[:, band], position * col_count, col_count, axis=2
    )
    previous = jnp.concatenate([initial_cols[None], traj_cols[:-1]], axis=0)
    resid_cols = partial_cols + previous
    inner = width - keep
    state_cols = jnp.transpose(traj_cols[:, :, inner : inner + rows], (1, 2, 3, 0))

    flat_units = slot_unit.reshape(-1)
    slot_total = slot_unit.shape[1]
    filled = (jnp.arange(slot_total, dtype=jnp.int32)[None, :] < unit_count[:, None]).reshape(-1)
    forward_table, inverse_table = slot_tables(flat_units, filled, step_count)

    outgoing = jnp.einsum(
        "tsp,tfyx->spfyx", forward_table, resid_cols, precision=lax.Precision.HIGH
    )
    pads = ((0, 0), (0, 0), (0, 0), (keep, keep), (0, 0))
    slot_share = outgoing.shape[0] // groups
    received = lax.all_to_all(
        outgoing.reshape((groups, slot_share) + outgoing.shape[1:]), "tm", 0, 0, tiled=False
    )
    owned = jnp.transpose(received, (1, 3, 2, 4, 0, 5))
    owned = owned.reshape(owned.shape[:4] + (-1,))
    wide_source = jnp.pad(owned, pads)

    own_units = lax.dynamic_index_in_dim(slot_unit, position, 0, keepdims=False)
    own_filled = lax.dynamic_index_in_dim(filled.reshape(groups, -1), position, 0, keepdims=False)
    coeffs = unit_inverse(own_units, step_count)

    global_row = lat_pos * rows - width + jnp.arange(rows + 2 * width, dtype=jnp.int32)
    row_mask = ((global_row >= 0) & (global_row < rows * lat_count)).astype(jnp.float32)
    solved = chebyshev(wide_source, wide_start, wide_depth, coeffs, row_mask[:, None])
    solved = solved[:, :, :, width : width + rows]
    spectrum = jnp.where(own_filled[:, None, None, None, None], solved, 0.0)

    sent = solved.reshape(solved.shape[:4] + (groups, -1))
    sent = jnp.transpose(sent, (4, 0, 2, 1, 3, 5))
    solved_cols = lax.all_to_all(sent, "tm", 0, 0, tiled=False)
    solved_cols = solved_cols.reshape((-1,) + solved_cols.shape[2:])
    corr = jnp.einsum(
        "spfyx,tsp->fyxt", solved_cols, inverse_table, precision=lax.Precision.HIGH
    )
    updated = state_cols + corr
    return (updated, spectrum)


def solution(mesh):
    return jax.shard_map(
        body,
        mesh=mesh,
        in_specs=(
            P("tm", None, "lat", None),
            P("tm", None, "lat", None),
            P(None, "lat", None),
            P("lat", None),
            P("tm", None, None, "lat", None),
            P(),
            P(),
        ),
        out_specs=(P(None, "lat", "tm", None), P("tm", None, None, "lat", None)),
        check_vma=False,
    )
```

```python
import math

import jax
import jax.numpy as jnp
from jax import lax
from jax.sharding import PartitionSpec as P

SWEEPS = 6


HALF_COUPLING = 0.125
CORIOLIS = 0.2
FRICTION = 1.0
ALPHA = 0.1
SPREAD = 0.2


def with_halo(cells, sides, width):
    for axis, dim in sides:
        count = lax.axis_size(axis)
        ends = count - 1
        head = lax.slice_in_dim(cells, 0, width, axis=dim)
        tail = lax.slice_in_dim(cells, cells.shape[dim] - width, cells.shape[dim], axis=dim)
        cells = jnp.concatenate(
            [
                lax.ppermute(tail, axis, [(i, (i + 1) % count) for i in range(ends)]),
                cells,
                lax.ppermute(head, axis, [((i + 1) % count, i) for i in range(ends)]),
            ],
            axis=dim,
        )
    return cells


def shifted(value, axis, by):
    size = lax.axis_size(axis)
    pairs = [(i, i + by) for i in range(size) if 0 <= i + by < size]
    return lax.ppermute(value, axis, pairs)


def flux_operator(state, depth, pad_rule, row_mask=None):
    height = state[..., 0:1, :, :, :]
    east = state[..., 1:2, :, :, :]
    north = state[..., 2:3, :, :, :]
    if row_mask is not None:
        height = height * row_mask
    flux = jnp.concatenate([height, depth * east, depth * north], axis=-4)
    padded = pad_rule(flux)
    grad_x = padded[..., 0:1, :, 1:-1, 2:] - padded[..., 0:1, :, 1:-1, :-2]
    grad_y = padded[..., 0:1, :, 2:, 1:-1] - padded[..., 0:1, :, :-2, 1:-1]
    diverge = (
        padded[..., 1:2, :, 1:-1, 2:]
        - padded[..., 1:2, :, 1:-1, :-2]
        + (padded[..., 2:3, :, 2:, 1:-1] - padded[..., 2:3, :, :-2, 1:-1])
    )
    new_height = HALF_COUPLING * diverge
    new_east = HALF_COUPLING * grad_x - CORIOLIS * north
    new_north = HALF_COUPLING * grad_y + CORIOLIS * east
    return jnp.concatenate([new_height, new_east, new_north], axis=-4)


def row_rims(flux):
    rows_done = with_halo(flux, (("lat", 3),), 1)
    return jnp.pad(rows_done, ((0, 0), (0, 0), (0, 0), (0, 0), (1, 1)))


def zero_rim(values):
    widths = [(0, 0)] * (values.ndim - 2) + [(1, 1), (1, 1)]
    return jnp.pad(values, widths)


def to_owners(slots):
    return lax.all_to_all(slots, "tm", split_axis=0, concat_axis=4, tiled=True)


def from_owners(slots):
    return lax.all_to_all(slots, "tm", split_axis=4, concat_axis=0, tiled=True)


def slot_tables(units, filled, step_count):
    index_t = jnp.arange(step_count, dtype=jnp.int32)
    phases = index_t[:, None] * units[None, :] % step_count
    angles = phases.astype(jnp.float32) * (2.0 * math.pi / step_count)
    cosine = jnp.cos(angles)
    sine = jnp.sin(angles)
    parity = (1 - 2 * (index_t % 2)).astype(jnp.float32)
    first = units == 0
    times = index_t.astype(jnp.float32) / step_count
    damping = jnp.exp(times * math.log(ALPHA)) / math.sqrt(step_count)
    growth = jnp.exp(-times * math.log(ALPHA)) / math.sqrt(step_count)
    forward_imag = jnp.where(first[None, :], parity[:, None], -sine)
    forward_table = jnp.stack([cosine, forward_imag], axis=2) * damping[:, None, None]
    weights = jnp.where(first, 1.0, 2.0).astype(jnp.float32)
    inverse_real = cosine * weights[None, :]
    inverse_imag = jnp.where(first[None, :], parity[:, None], -2.0 * sine)
    keep = filled.astype(jnp.float32)[None, :, None]
    inverse_table = jnp.stack([inverse_real, inverse_imag], axis=2) * growth[:, None, None] * keep
    return (forward_table, inverse_table)


def unit_inverse(pair_ids, step_count):
    angles = pair_ids.astype(jnp.float32) * (2.0 * math.pi / step_count)
    ratio = math.exp(math.log(ALPHA) / step_count)
    real_shift = 1.0 + FRICTION - ratio * jnp.cos(angles)
    imag_shift = ratio * jnp.sin(angles)
    denominator = real_shift * real_shift + imag_shift * imag_shift
    real_inv = real_shift / denominator
    imag_inv = -imag_shift / denominator
    is_first = pair_ids == 0
    upper_left = jnp.where(is_first, 1.0 / (1.0 + FRICTION - ratio), real_inv)
    upper_right = jnp.where(is_first, 0.0, -imag_inv)
    lower_left = jnp.where(is_first, 0.0, imag_inv)
    lower_right = jnp.where(is_first, 1.0 / (1.0 + FRICTION + ratio), real_inv)
    return (upper_left, upper_right, lower_left, lower_right)


def apply_inverse(coeffs, values):
    shaped = [c[:, None, None, None] for c in coeffs]
    real_part = values[:, :, 0]
    imag_part = values[:, :, 1]
    new_real = shaped[0] * real_part + shaped[1] * imag_part
    new_imag = shaped[2] * real_part + shaped[3] * imag_part
    return jnp.stack([new_real, new_imag], axis=2)


def chebyshev(source, start, depth, coeffs, row_mask):
    iterate = start
    for sweep in range(SWEEPS):
        weight = 1.0 / (1.0 + SPREAD * math.cos(math.pi * (2 * sweep + 1) / (2 * SWEEPS)))
        flux = flux_operator(iterate, depth, zero_rim, row_mask)
        update = apply_inverse(coeffs, source - flux) - iterate
        iterate = iterate + weight * update
    return iterate


def lat_halo(arrays, width, sent):
    flat = [a.reshape((-1,) + a.shape[-2:]) for a in arrays]
    packed = jnp.concatenate(flat, axis=0)
    rows = packed.shape[1]
    count = lax.axis_size("lat")
    above = lax.ppermute(packed[:, rows - sent :], "lat", [(i, i + 1) for i in range(count - 1)])
    below = lax.ppermute(packed[:, :sent], "lat", [(i + 1, i) for i in range(count - 1)])
    blank = jnp.zeros((packed.shape[0], width - sent, packed.shape[2]), packed.dtype)
    wide = jnp.concatenate([blank, above, packed, below, blank], axis=1)
    out, offset = [], 0
    for a, f in zip(arrays, flat):
        piece = wide[offset : offset + f.shape[0]]
        out.append(piece.reshape(a.shape[:-2] + piece.shape[1:]))
        offset += f.shape[0]
    return out


def body(trajectory, forcing, initial_state, depth, warm_start, slot_unit, unit_count):
    groups = lax.axis_size("tm")
    position = lax.axis_index("tm")
    local_steps = trajectory.shape[0]
    step_count = local_steps * groups
    rows = depth.shape[0]
    lat_count = lax.axis_size("lat")
    lat_pos = lax.axis_index("lat")
    width = 8 * ((SWEEPS + 7) // 8)

    wide_traj, wide_forcing, wide_initial, wide_depth = lat_halo(
        [trajectory, forcing, initial_state, depth], width, SWEEPS
    )
    flux_term = flux_operator(wide_traj[:, :, None], wide_depth, zero_rim)[:, :, 0]
    partial = wide_forcing - ((1.0 + FRICTION) * wide_traj + flux_term)
    keep = width - SWEEPS + 1
    band = slice(keep, rows + 2 * width - keep)
    outgoing_rows, warm_start = lax.optimization_barrier(
        (jnp.stack([wide_traj[:, :, band], partial[:, :, band]], axis=1), warm_start)
    )
    (wide_start,) = lat_halo([warm_start], width, SWEEPS)
    moved = lax.all_to_all(
        outgoing_rows,
        "tm",
        split_axis=4,
        concat_axis=0,
        tiled=True,
    )
    traj_cols, partial_cols = moved[:, 0], moved[:, 1]
    col_count = traj_cols.shape[3]
    initial_cols = lax.dynamic_slice_in_dim(
        wide_initial[:, band], position * col_count, col_count, axis=2
    )
    previous = jnp.concatenate([initial_cols[None], traj_cols[:-1]], axis=0)
    resid_cols = partial_cols + previous
    inner = width - keep
    state_cols = jnp.transpose(traj_cols[:, :, inner : inner + rows], (1, 2, 3, 0))

    flat_units = slot_unit.reshape(-1)
    slot_total = slot_unit.shape[1]
    filled = (jnp.arange(slot_total, dtype=jnp.int32)[None, :] < unit_count[:, None]).reshape(-1)
    forward_table, inverse_table = slot_tables(flat_units, filled, step_count)

    outgoing = jnp.einsum(
        "tsp,tfyx->spfyx", forward_table, resid_cols, precision=lax.Precision.HIGH
    )
    pads = ((0, 0), (0, 0), (0, 0), (keep, keep), (0, 0))
    wide_source = jnp.pad(jnp.transpose(to_owners(outgoing), (0, 2, 1, 3, 4)), pads)

    own_units = lax.dynamic_index_in_dim(slot_unit, position, 0, keepdims=False)
    own_filled = lax.dynamic_index_in_dim(filled.reshape(groups, -1), position, 0, keepdims=False)
    coeffs = unit_inverse(own_units, step_count)

    global_row = lat_pos * rows - width + jnp.arange(rows + 2 * width, dtype=jnp.int32)
    row_mask = ((global_row >= 0) & (global_row < rows * lat_count)).astype(jnp.float32)
    solved = chebyshev(wide_source, wide_start, wide_depth, coeffs, row_mask[:, None])
    solved = solved[:, :, :, width : width + rows]
    spectrum = jnp.where(own_filled[:, None, None, None, None], solved, 0.0)

    solved_cols = from_owners(jnp.transpose(solved, (0, 2, 1, 3, 4)))
    corr = jnp.einsum(
        "spfyx,tsp->fyxt", solved_cols, inverse_table, precision=lax.Precision.HIGH
    )
    updated = state_cols + corr
    return (updated, spectrum)


def solution(mesh):
    return jax.shard_map(
        body,
        mesh=mesh,
        in_specs=(
            P("tm", None, "lat", None),
            P("tm", None, "lat", None),
            P(None, "lat", None),
            P("lat", None),
            P("tm", None, None, "lat", None),
            P(),
            P(),
        ),
        out_specs=(P(None, "lat", "tm", None), P("tm", None, None, "lat", None)),
        check_vma=False,
    )
```

```python
import math

import jax
import jax.numpy as jnp
from jax import lax
from jax.sharding import PartitionSpec as P

SWEEPS = 6


HALF_COUPLING = 0.125
CORIOLIS = 0.2
FRICTION = 1.0
ALPHA = 0.1
SPREAD = 0.2


def with_halo(cells, sides, width):
    for axis, dim in sides:
        count = lax.axis_size(axis)
        ends = count - 1
        head = lax.slice_in_dim(cells, 0, width, axis=dim)
        tail = lax.slice_in_dim(cells, cells.shape[dim] - width, cells.shape[dim], axis=dim)
        cells = jnp.concatenate(
            [
                lax.ppermute(tail, axis, [(i, (i + 1) % count) for i in range(ends)]),
                cells,
                lax.ppermute(head, axis, [((i + 1) % count, i) for i in range(ends)]),
            ],
            axis=dim,
        )
    return cells


def shifted(value, axis, by):
    size = lax.axis_size(axis)
    pairs = [(i, i + by) for i in range(size) if 0 <= i + by < size]
    return lax.ppermute(value, axis, pairs)


def flux_operator(state, depth, pad_rule, row_mask=None):
    height = state[..., 0:1, :, :, :]
    east = state[..., 1:2, :, :, :]
    north = state[..., 2:3, :, :, :]
    if row_mask is not None:
        height = height * row_mask
    flux = jnp.concatenate([height, depth * east, depth * north], axis=-4)
    padded = pad_rule(flux)
    grad_x = padded[..., 0:1, :, 1:-1, 2:] - padded[..., 0:1, :, 1:-1, :-2]
    grad_y = padded[..., 0:1, :, 2:, 1:-1] - padded[..., 0:1, :, :-2, 1:-1]
    diverge = (
        padded[..., 1:2, :, 1:-1, 2:]
        - padded[..., 1:2, :, 1:-1, :-2]
        + (padded[..., 2:3, :, 2:, 1:-1] - padded[..., 2:3, :, :-2, 1:-1])
    )
    new_height = HALF_COUPLING * diverge
    new_east = HALF_COUPLING * grad_x - CORIOLIS * north
    new_north = HALF_COUPLING * grad_y + CORIOLIS * east
    return jnp.concatenate([new_height, new_east, new_north], axis=-4)


def row_rims(flux):
    rows_done = with_halo(flux, (("lat", 3),), 1)
    return jnp.pad(rows_done, ((0, 0), (0, 0), (0, 0), (0, 0), (1, 1)))


def zero_rim(values):
    widths = [(0, 0)] * (values.ndim - 2) + [(1, 1), (1, 1)]
    return jnp.pad(values, widths)


def to_owners(slots):
    return lax.all_to_all(slots, "tm", split_axis=0, concat_axis=4, tiled=True)


def from_owners(slots):
    return lax.all_to_all(slots, "tm", split_axis=4, concat_axis=0, tiled=True)


def slot_tables(units, filled, step_count):
    index_t = jnp.arange(step_count, dtype=jnp.int32)
    phases = index_t[:, None] * units[None, :] % step_count
    angles = phases.astype(jnp.float32) * (2.0 * math.pi / step_count)
    cosine = jnp.cos(angles)
    sine = jnp.sin(angles)
    parity = (1 - 2 * (index_t % 2)).astype(jnp.float32)
    first = units == 0
    times = index_t.astype(jnp.float32) / step_count
    damping = jnp.exp(times * math.log(ALPHA)) / math.sqrt(step_count)
    growth = jnp.exp(-times * math.log(ALPHA)) / math.sqrt(step_count)
    forward_imag = jnp.where(first[None, :], parity[:, None], -sine)
    forward_table = jnp.stack([cosine, forward_imag], axis=2) * damping[:, None, None]
    weights = jnp.where(first, 1.0, 2.0).astype(jnp.float32)
    inverse_real = cosine * weights[None, :]
    inverse_imag = jnp.where(first[None, :], parity[:, None], -2.0 * sine)
    keep = filled.astype(jnp.float32)[None, :, None]
    inverse_table = jnp.stack([inverse_real, inverse_imag], axis=2) * growth[:, None, None] * keep
    return (forward_table, inverse_table)


def unit_inverse(pair_ids, step_count):
    angles = pair_ids.astype(jnp.float32) * (2.0 * math.pi / step_count)
    ratio = math.exp(math.log(ALPHA) / step_count)
    real_shift = 1.0 + FRICTION - ratio * jnp.cos(angles)
    imag_shift = ratio * jnp.sin(angles)
    denominator = real_shift * real_shift + imag_shift * imag_shift
    real_inv = real_shift / denominator
    imag_inv = -imag_shift / denominator
    is_first = pair_ids == 0
    upper_left = jnp.where(is_first, 1.0 / (1.0 + FRICTION - ratio), real_inv)
    upper_right = jnp.where(is_first, 0.0, -imag_inv)
    lower_left = jnp.where(is_first, 0.0, imag_inv)
    lower_right = jnp.where(is_first, 1.0 / (1.0 + FRICTION + ratio), real_inv)
    return (upper_left, upper_right, lower_left, lower_right)


def apply_inverse(coeffs, values):
    shaped = [c[:, None, None, None] for c in coeffs]
    real_part = values[:, :, 0]
    imag_part = values[:, :, 1]
    new_real = shaped[0] * real_part + shaped[1] * imag_part
    new_imag = shaped[2] * real_part + shaped[3] * imag_part
    return jnp.stack([new_real, new_imag], axis=2)


def chebyshev(source, start, depth, coeffs, row_mask):
    iterate = start
    for sweep in range(SWEEPS):
        weight = 1.0 / (1.0 + SPREAD * math.cos(math.pi * (2 * sweep + 1) / (2 * SWEEPS)))
        flux = flux_operator(iterate, depth, zero_rim, row_mask)
        update = apply_inverse(coeffs, source - flux) - iterate
        iterate = iterate + weight * update
    return iterate


def lat_halo(arrays, width, sent):
    flat = [a.reshape((-1,) + a.shape[-2:]) for a in arrays]
    packed = jnp.concatenate(flat, axis=0)
    rows = packed.shape[1]
    count = lax.axis_size("lat")
    above = lax.ppermute(packed[:, rows - sent :], "lat", [(i, i + 1) for i in range(count - 1)])
    below = lax.ppermute(packed[:, :sent], "lat", [(i + 1, i) for i in range(count - 1)])
    blank = jnp.zeros((packed.shape[0], width - sent, packed.shape[2]), packed.dtype)
    wide = jnp.concatenate([blank, above, packed, below, blank], axis=1)
    out, offset = [], 0
    for a, f in zip(arrays, flat):
        piece = wide[offset : offset + f.shape[0]]
        out.append(piece.reshape(a.shape[:-2] + piece.shape[1:]))
        offset += f.shape[0]
    return out


def body(trajectory, forcing, initial_state, depth, warm_start, slot_unit, unit_count):
    groups = lax.axis_size("tm")
    position = lax.axis_index("tm")
    local_steps = trajectory.shape[0]
    step_count = local_steps * groups
    rows = depth.shape[0]
    lat_count = lax.axis_size("lat")
    lat_pos = lax.axis_index("lat")
    width = 8 * ((SWEEPS + 7) // 8)

    wide_traj, wide_forcing, wide_initial, wide_depth = lat_halo(
        [trajectory, forcing, initial_state, depth], width, SWEEPS
    )
    flux_term = flux_operator(wide_traj[:, :, None], wide_depth, zero_rim)[:, :, 0]
    partial = wide_forcing - ((1.0 + FRICTION) * wide_traj + flux_term)
    keep = width - SWEEPS + 1
    band = slice(keep, rows + 2 * width - keep)
    band_traj = wide_traj[:, :, band]
    band_part = partial[:, :, band]
    payload = jnp.concatenate(
        [
            wide_traj[0, :, width : width + rows],
            band_traj[1],
            band_part[0],
            band_part[1] + band_traj[0],
        ],
        axis=1,
    )
    outgoing_rows, warm_start = lax.optimization_barrier((payload[None], warm_start))
    (wide_start,) = lat_halo([warm_start], width, SWEEPS)
    moved = lax.all_to_all(outgoing_rows, "tm", split_axis=3, concat_axis=0, tiled=True)
    band_rows = band_traj.shape[2]
    first = moved[:, :, :rows]
    second = moved[:, :, rows : rows + band_rows]
    even_part = moved[:, :, rows + band_rows : rows + 2 * band_rows]
    odd_resid = moved[:, :, rows + 2 * band_rows :]
    col_count = moved.shape[3]
    initial_cols = lax.dynamic_slice_in_dim(
        wide_initial[:, band], position * col_count, col_count, axis=2
    )
    previous = jnp.concatenate([initial_cols[None], second[:-1]], axis=0)
    resid_cols = jnp.stack([even_part + previous, odd_resid], axis=1)
    resid_cols = resid_cols.reshape((-1,) + resid_cols.shape[2:])
    inner = width - keep
    state_cols = jnp.stack([first, second[:, :, inner : inner + rows]], axis=1)
    state_cols = jnp.transpose(state_cols.reshape((-1,) + state_cols.shape[2:]), (1, 2, 3, 0))

    flat_units = slot_unit.reshape(-1)
    slot_total = slot_unit.shape[1]
    filled = (jnp.arange(slot_total, dtype=jnp.int32)[None, :] < unit_count[:, None]).reshape(-1)
    forward_table, inverse_table = slot_tables(flat_units, filled, step_count)

    outgoing = jnp.einsum(
        "tsp,tfyx->spfyx", forward_table, resid_cols, precision=lax.Precision.HIGH
    )
    pads = ((0, 0), (0, 0), (0, 0), (keep, keep), (0, 0))
    wide_source = jnp.pad(jnp.transpose(to_owners(outgoing), (0, 2, 1, 3, 4)), pads)

    own_units = lax.dynamic_index_in_dim(slot_unit, position, 0, keepdims=False)
    own_filled = lax.dynamic_index_in_dim(filled.reshape(groups, -1), position, 0, keepdims=False)
    coeffs = unit_inverse(own_units, step_count)

    global_row = lat_pos * rows - width + jnp.arange(rows + 2 * width, dtype=jnp.int32)
    row_mask = ((global_row >= 0) & (global_row < rows * lat_count)).astype(jnp.float32)
    solved = chebyshev(wide_source, wide_start, wide_depth, coeffs, row_mask[:, None])
    solved = solved[:, :, :, width : width + rows]
    spectrum = jnp.where(own_filled[:, None, None, None, None], solved, 0.0)

    solved_cols = from_owners(jnp.transpose(solved, (0, 2, 1, 3, 4)))
    corr = jnp.einsum(
        "spfyx,tsp->fyxt", solved_cols, inverse_table, precision=lax.Precision.HIGH
    )
    updated = state_cols + corr
    return (updated, spectrum)


def solution(mesh):
    return jax.shard_map(
        body,
        mesh=mesh,
        in_specs=(
            P("tm", None, "lat", None),
            P("tm", None, "lat", None),
            P(None, "lat", None),
            P("lat", None),
            P("tm", None, None, "lat", None),
            P(),
            P(),
        ),
        out_specs=(P(None, "lat", "tm", None), P("tm", None, None, "lat", None)),
        check_vma=False,
    )
```

```python
import math

import jax
import jax.numpy as jnp
from jax import lax
from jax.sharding import PartitionSpec as P

SWEEPS = 6


HALF_COUPLING = 0.125
CORIOLIS = 0.2
FRICTION = 1.0
ALPHA = 0.1
SPREAD = 0.2


def with_halo(cells, sides, width):
    for axis, dim in sides:
        count = lax.axis_size(axis)
        ends = count - 1
        head = lax.slice_in_dim(cells, 0, width, axis=dim)
        tail = lax.slice_in_dim(cells, cells.shape[dim] - width, cells.shape[dim], axis=dim)
        cells = jnp.concatenate(
            [
                lax.ppermute(tail, axis, [(i, (i + 1) % count) for i in range(ends)]),
                cells,
                lax.ppermute(head, axis, [((i + 1) % count, i) for i in range(ends)]),
            ],
            axis=dim,
        )
    return cells


def shifted(value, axis, by):
    size = lax.axis_size(axis)
    pairs = [(i, i + by) for i in range(size) if 0 <= i + by < size]
    return lax.ppermute(value, axis, pairs)


def flux_operator(state, depth, pad_rule, row_mask=None):
    height = state[..., 0:1, :, :, :]
    east = state[..., 1:2, :, :, :]
    north = state[..., 2:3, :, :, :]
    if row_mask is not None:
        height = height * row_mask
    flux = jnp.concatenate([height, depth * east, depth * north], axis=-4)
    padded = pad_rule(flux)
    grad_x = padded[..., 0:1, :, 1:-1, 2:] - padded[..., 0:1, :, 1:-1, :-2]
    grad_y = padded[..., 0:1, :, 2:, 1:-1] - padded[..., 0:1, :, :-2, 1:-1]
    diverge = (
        padded[..., 1:2, :, 1:-1, 2:]
        - padded[..., 1:2, :, 1:-1, :-2]
        + (padded[..., 2:3, :, 2:, 1:-1] - padded[..., 2:3, :, :-2, 1:-1])
    )
    new_height = HALF_COUPLING * diverge
    new_east = HALF_COUPLING * grad_x - CORIOLIS * north
    new_north = HALF_COUPLING * grad_y + CORIOLIS * east
    return jnp.concatenate([new_height, new_east, new_north], axis=-4)


def row_rims(flux):
    rows_done = with_halo(flux, (("lat", 3),), 1)
    return jnp.pad(rows_done, ((0, 0), (0, 0), (0, 0), (0, 0), (1, 1)))


def zero_rim(values):
    widths = [(0, 0)] * (values.ndim - 2) + [(1, 1), (1, 1)]
    return jnp.pad(values, widths)


def to_owners(slots):
    return lax.all_to_all(slots, "tm", split_axis=0, concat_axis=4, tiled=True)


def from_owners(slots):
    return lax.all_to_all(slots, "tm", split_axis=4, concat_axis=0, tiled=True)


def slot_tables(units, filled, step_count):
    index_t = jnp.arange(step_count, dtype=jnp.int32)
    phases = index_t[:, None] * units[None, :] % step_count
    angles = phases.astype(jnp.float32) * (2.0 * math.pi / step_count)
    cosine = jnp.cos(angles)
    sine = jnp.sin(angles)
    parity = (1 - 2 * (index_t % 2)).astype(jnp.float32)
    first = units == 0
    times = index_t.astype(jnp.float32) / step_count
    damping = jnp.exp(times * math.log(ALPHA)) / math.sqrt(step_count)
    growth = jnp.exp(-times * math.log(ALPHA)) / math.sqrt(step_count)
    forward_imag = jnp.where(first[None, :], parity[:, None], -sine)
    forward_table = jnp.stack([cosine, forward_imag], axis=2) * damping[:, None, None]
    weights = jnp.where(first, 1.0, 2.0).astype(jnp.float32)
    inverse_real = cosine * weights[None, :]
    inverse_imag = jnp.where(first[None, :], parity[:, None], -2.0 * sine)
    keep = filled.astype(jnp.float32)[None, :, None]
    inverse_table = jnp.stack([inverse_real, inverse_imag], axis=2) * growth[:, None, None] * keep
    return (forward_table, inverse_table)


def unit_inverse(pair_ids, step_count):
    angles = pair_ids.astype(jnp.float32) * (2.0 * math.pi / step_count)
    ratio = math.exp(math.log(ALPHA) / step_count)
    real_shift = 1.0 + FRICTION - ratio * jnp.cos(angles)
    imag_shift = ratio * jnp.sin(angles)
    denominator = real_shift * real_shift + imag_shift * imag_shift
    real_inv = real_shift / denominator
    imag_inv = -imag_shift / denominator
    is_first = pair_ids == 0
    upper_left = jnp.where(is_first, 1.0 / (1.0 + FRICTION - ratio), real_inv)
    upper_right = jnp.where(is_first, 0.0, -imag_inv)
    lower_left = jnp.where(is_first, 0.0, imag_inv)
    lower_right = jnp.where(is_first, 1.0 / (1.0 + FRICTION + ratio), real_inv)
    return (upper_left, upper_right, lower_left, lower_right)


def apply_inverse(coeffs, values):
    shaped = [c[:, None, None, None] for c in coeffs]
    real_part = values[:, :, 0]
    imag_part = values[:, :, 1]
    new_real = shaped[0] * real_part + shaped[1] * imag_part
    new_imag = shaped[2] * real_part + shaped[3] * imag_part
    return jnp.stack([new_real, new_imag], axis=2)


def chebyshev(source, start, depth, coeffs, row_mask):
    iterate = start
    for sweep in range(SWEEPS):
        weight = 1.0 / (1.0 + SPREAD * math.cos(math.pi * (2 * sweep + 1) / (2 * SWEEPS)))
        flux = flux_operator(iterate, depth, zero_rim, row_mask)
        update = apply_inverse(coeffs, source - flux) - iterate
        iterate = iterate + weight * update
    return iterate


def lat_halo(arrays, width, sent):
    flat = [a.reshape((-1,) + a.shape[-2:]) for a in arrays]
    packed = jnp.concatenate(flat, axis=0)
    rows = packed.shape[1]
    count = lax.axis_size("lat")
    above = lax.ppermute(packed[:, rows - sent :], "lat", [(i, i + 1) for i in range(count - 1)])
    below = lax.ppermute(packed[:, :sent], "lat", [(i + 1, i) for i in range(count - 1)])
    blank = jnp.zeros((packed.shape[0], width - sent, packed.shape[2]), packed.dtype)
    wide = jnp.concatenate([blank, above, packed, below, blank], axis=1)
    out, offset = [], 0
    for a, f in zip(arrays, flat):
        piece = wide[offset : offset + f.shape[0]]
        out.append(piece.reshape(a.shape[:-2] + piece.shape[1:]))
        offset += f.shape[0]
    return out


def body(trajectory, forcing, initial_state, depth, warm_start, slot_unit, unit_count):
    groups = lax.axis_size("tm")
    position = lax.axis_index("tm")
    local_steps = trajectory.shape[0]
    step_count = local_steps * groups
    rows = depth.shape[0]
    lat_count = lax.axis_size("lat")
    lat_pos = lax.axis_index("lat")
    width = 8 * ((SWEEPS + 7) // 8)

    wide_traj, wide_forcing, wide_initial, wide_depth = lat_halo(
        [trajectory, forcing, initial_state, depth], width, SWEEPS
    )
    flux_term = flux_operator(wide_traj[:, :, None], wide_depth, zero_rim)[:, :, 0]
    partial = wide_forcing - ((1.0 + FRICTION) * wide_traj + flux_term)
    keep = width - SWEEPS + 1
    band = slice(keep, rows + 2 * width - keep)
    band_traj = wide_traj[:, :, band]
    band_part = partial[:, :, band]
    payload = jnp.concatenate(
        [
            wide_traj[0, :, width : width + rows],
            band_traj[1],
            band_part[0],
            band_part[1] + band_traj[0],
        ],
        axis=1,
    )
    outgoing_rows, warm_start = lax.optimization_barrier((payload[None], warm_start))
    (wide_start,) = lat_halo([warm_start], width, SWEEPS)
    moved = lax.all_to_all(outgoing_rows, "tm", split_axis=3, concat_axis=0, tiled=True)
    band_rows = band_traj.shape[2]
    first = moved[:, :, :rows]
    second = moved[:, :, rows : rows + band_rows]
    even_part = moved[:, :, rows + band_rows : rows + 2 * band_rows]
    odd_resid = moved[:, :, rows + 2 * band_rows :]
    col_count = moved.shape[3]
    initial_cols = lax.dynamic_slice_in_dim(
        wide_initial[:, band], position * col_count, col_count, axis=2
    )
    previous = jnp.concatenate([initial_cols[None], second[:-1]], axis=0)
    resid_cols = jnp.stack([even_part + previous, odd_resid], axis=1)
    resid_cols = resid_cols.reshape((-1,) + resid_cols.shape[2:])
    inner = width - keep
    state_cols = jnp.stack([first, second[:, :, inner : inner + rows]], axis=1)
    state_cols = jnp.transpose(state_cols.reshape((-1,) + state_cols.shape[2:]), (1, 2, 3, 0))

    flat_units = slot_unit.reshape(-1)
    slot_total = slot_unit.shape[1]
    filled = (jnp.arange(slot_total, dtype=jnp.int32)[None, :] < unit_count[:, None]).reshape(-1)
    forward_table, inverse_table = slot_tables(flat_units, filled, step_count)

    outgoing = jnp.einsum(
        "tsp,tfyx->spfyx", forward_table, resid_cols, precision=lax.Precision.HIGH
    )
    pads = ((0, 0), (0, 0), (0, 0), (keep, keep), (0, 0))
    wide_source = jnp.pad(jnp.transpose(to_owners(outgoing), (0, 2, 1, 3, 4)), pads)

    own_units = lax.dynamic_index_in_dim(slot_unit, position, 0, keepdims=False)
    own_filled = lax.dynamic_index_in_dim(filled.reshape(groups, -1), position, 0, keepdims=False)
    coeffs = unit_inverse(own_units, step_count)

    global_row = lat_pos * rows - width + jnp.arange(rows + 2 * width, dtype=jnp.int32)
    row_mask = ((global_row >= 0) & (global_row < rows * lat_count)).astype(jnp.float32)
    solved = chebyshev(wide_source, wide_start, wide_depth, coeffs, row_mask[:, None])
    solved = solved[:, :, :, width : width + rows]
    spectrum = jnp.where(own_filled[:, None, None, None, None], solved, 0.0)

    solved_cols = lax.all_to_all(
        jnp.transpose(solved, (0, 2, 1, 3, 4))[None], "tm", split_axis=5, concat_axis=0, tiled=True
    )
    solved_cols = solved_cols.reshape((-1,) + solved_cols.shape[2:])
    corr = jnp.einsum(
        "spfyx,tsp->fyxt", solved_cols, inverse_table, precision=lax.Precision.HIGH
    )
    updated = state_cols + corr
    return (updated, spectrum)


def solution(mesh):
    return jax.shard_map(
        body,
        mesh=mesh,
        in_specs=(
            P("tm", None, "lat", None),
            P("tm", None, "lat", None),
            P(None, "lat", None),
            P("lat", None),
            P("tm", None, None, "lat", None),
            P(),
            P(),
        ),
        out_specs=(P(None, "lat", "tm", None), P("tm", None, None, "lat", None)),
        check_vma=False,
    )
```

```python
import math

import jax
import jax.numpy as jnp
from jax import lax
from jax.sharding import PartitionSpec as P

SWEEPS = 6


HALF_COUPLING = 0.125
CORIOLIS = 0.2
FRICTION = 1.0
ALPHA = 0.1
SPREAD = 0.2


def with_halo(cells, sides, width):
    for axis, dim in sides:
        count = lax.axis_size(axis)
        ends = count - 1
        head = lax.slice_in_dim(cells, 0, width, axis=dim)
        tail = lax.slice_in_dim(cells, cells.shape[dim] - width, cells.shape[dim], axis=dim)
        cells = jnp.concatenate(
            [
                lax.ppermute(tail, axis, [(i, (i + 1) % count) for i in range(ends)]),
                cells,
                lax.ppermute(head, axis, [((i + 1) % count, i) for i in range(ends)]),
            ],
            axis=dim,
        )
    return cells


def shifted(value, axis, by):
    size = lax.axis_size(axis)
    pairs = [(i, i + by) for i in range(size) if 0 <= i + by < size]
    return lax.ppermute(value, axis, pairs)


def flux_operator(state, depth, pad_rule, row_mask=None):
    height = state[..., 0:1, :, :, :]
    east = state[..., 1:2, :, :, :]
    north = state[..., 2:3, :, :, :]
    if row_mask is not None:
        height = height * row_mask
    flux = jnp.concatenate([height, depth * east, depth * north], axis=-4)
    padded = pad_rule(flux)
    grad_x = padded[..., 0:1, :, 1:-1, 2:] - padded[..., 0:1, :, 1:-1, :-2]
    grad_y = padded[..., 0:1, :, 2:, 1:-1] - padded[..., 0:1, :, :-2, 1:-1]
    diverge = (
        padded[..., 1:2, :, 1:-1, 2:]
        - padded[..., 1:2, :, 1:-1, :-2]
        + (padded[..., 2:3, :, 2:, 1:-1] - padded[..., 2:3, :, :-2, 1:-1])
    )
    new_height = HALF_COUPLING * diverge
    new_east = HALF_COUPLING * grad_x - CORIOLIS * north
    new_north = HALF_COUPLING * grad_y + CORIOLIS * east
    return jnp.concatenate([new_height, new_east, new_north], axis=-4)


def row_rims(flux):
    rows_done = with_halo(flux, (("lat", 3),), 1)
    return jnp.pad(rows_done, ((0, 0), (0, 0), (0, 0), (0, 0), (1, 1)))


def zero_rim(values):
    widths = [(0, 0)] * (values.ndim - 2) + [(1, 1), (1, 1)]
    return jnp.pad(values, widths)


def to_owners(slots):
    return lax.all_to_all(slots, "tm", split_axis=0, concat_axis=4, tiled=True)


def from_owners(slots):
    return lax.all_to_all(slots, "tm", split_axis=4, concat_axis=0, tiled=True)


def slot_tables(units, filled, step_count):
    index_t = jnp.arange(step_count, dtype=jnp.int32)
    phases = index_t[:, None] * units[None, :] % step_count
    angles = phases.astype(jnp.float32) * (2.0 * math.pi / step_count)
    cosine = jnp.cos(angles)
    sine = jnp.sin(angles)
    parity = (1 - 2 * (index_t % 2)).astype(jnp.float32)
    first = units == 0
    times = index_t.astype(jnp.float32) / step_count
    damping = jnp.exp(times * math.log(ALPHA)) / math.sqrt(step_count)
    growth = jnp.exp(-times * math.log(ALPHA)) / math.sqrt(step_count)
    forward_imag = jnp.where(first[None, :], parity[:, None], -sine)
    forward_table = jnp.stack([cosine, forward_imag], axis=2) * damping[:, None, None]
    weights = jnp.where(first, 1.0, 2.0).astype(jnp.float32)
    inverse_real = cosine * weights[None, :]
    inverse_imag = jnp.where(first[None, :], parity[:, None], -2.0 * sine)
    keep = filled.astype(jnp.float32)[None, :, None]
    inverse_table = jnp.stack([inverse_real, inverse_imag], axis=2) * growth[:, None, None] * keep
    return (forward_table, inverse_table)


def unit_inverse(pair_ids, step_count):
    angles = pair_ids.astype(jnp.float32) * (2.0 * math.pi / step_count)
    ratio = math.exp(math.log(ALPHA) / step_count)
    real_shift = 1.0 + FRICTION - ratio * jnp.cos(angles)
    imag_shift = ratio * jnp.sin(angles)
    denominator = real_shift * real_shift + imag_shift * imag_shift
    real_inv = real_shift / denominator
    imag_inv = -imag_shift / denominator
    is_first = pair_ids == 0
    upper_left = jnp.where(is_first, 1.0 / (1.0 + FRICTION - ratio), real_inv)
    upper_right = jnp.where(is_first, 0.0, -imag_inv)
    lower_left = jnp.where(is_first, 0.0, imag_inv)
    lower_right = jnp.where(is_first, 1.0 / (1.0 + FRICTION + ratio), real_inv)
    return (upper_left, upper_right, lower_left, lower_right)


def apply_inverse(coeffs, values):
    shaped = [c[:, None, None, None] for c in coeffs]
    real_part = values[:, :, 0]
    imag_part = values[:, :, 1]
    new_real = shaped[0] * real_part + shaped[1] * imag_part
    new_imag = shaped[2] * real_part + shaped[3] * imag_part
    return jnp.stack([new_real, new_imag], axis=2)


def chebyshev(source, start, depth, coeffs, row_mask):
    iterate = start
    for sweep in range(SWEEPS):
        weight = 1.0 / (1.0 + SPREAD * math.cos(math.pi * (2 * sweep + 1) / (2 * SWEEPS)))
        flux = flux_operator(iterate, depth, zero_rim, row_mask)
        update = apply_inverse(coeffs, source - flux) - iterate
        iterate = iterate + weight * update
    return iterate


def lat_halo(arrays, width, sent):
    flat = [a.reshape((-1,) + a.shape[-2:]) for a in arrays]
    packed = jnp.concatenate(flat, axis=0)
    rows = packed.shape[1]
    count = lax.axis_size("lat")
    above = lax.ppermute(packed[:, rows - sent :], "lat", [(i, i + 1) for i in range(count - 1)])
    below = lax.ppermute(packed[:, :sent], "lat", [(i + 1, i) for i in range(count - 1)])
    blank = jnp.zeros((packed.shape[0], width - sent, packed.shape[2]), packed.dtype)
    wide = jnp.concatenate([blank, above, packed, below, blank], axis=1)
    out, offset = [], 0
    for a, f in zip(arrays, flat):
        piece = wide[offset : offset + f.shape[0]]
        out.append(piece.reshape(a.shape[:-2] + piece.shape[1:]))
        offset += f.shape[0]
    return out


def body(trajectory, forcing, initial_state, depth, warm_start, slot_unit, unit_count):
    groups = lax.axis_size("tm")
    position = lax.axis_index("tm")
    local_steps = trajectory.shape[0]
    step_count = local_steps * groups
    rows = depth.shape[0]
    lat_count = lax.axis_size("lat")
    lat_pos = lax.axis_index("lat")
    width = 8 * ((SWEEPS + 7) // 8)

    wide_traj, wide_forcing, wide_initial, wide_depth = lat_halo(
        [trajectory, forcing, initial_state, depth], width, SWEEPS
    )
    flux_term = flux_operator(wide_traj[:, :, None], wide_depth, zero_rim)[:, :, 0]
    partial = wide_forcing - ((1.0 + FRICTION) * wide_traj + flux_term)
    keep = width - SWEEPS + 1
    band = slice(keep, rows + 2 * width - keep)
    band_traj = wide_traj[:, :, band]
    band_part = partial[:, :, band]
    payload = jnp.concatenate(
        [
            wide_traj[0, :, width : width + rows],
            band_traj[1],
            band_part[0],
            band_part[1] + band_traj[0],
        ],
        axis=1,
    )
    outgoing_rows, warm_start = lax.optimization_barrier((payload[None], warm_start))
    (wide_start,) = lat_halo([warm_start], width, SWEEPS)
    moved = lax.all_to_all(outgoing_rows, "tm", split_axis=3, concat_axis=0, tiled=True)
    band_rows = band_traj.shape[2]
    first = moved[:, :, :rows]
    second = moved[:, :, rows : rows + band_rows]
    even_part = moved[:, :, rows + band_rows : rows + 2 * band_rows]
    odd_resid = moved[:, :, rows + 2 * band_rows :]
    col_count = moved.shape[3]
    initial_cols = lax.dynamic_slice_in_dim(
        wide_initial[:, band], position * col_count, col_count, axis=2
    )
    previous = jnp.concatenate([initial_cols[None], second[:-1]], axis=0)
    resid_cols = jnp.stack([even_part + previous, odd_resid], axis=1)
    resid_cols = resid_cols.reshape((-1,) + resid_cols.shape[2:])
    inner = width - keep
    state_cols = jnp.stack([first, second[:, :, inner : inner + rows]], axis=1)
    state_cols = jnp.transpose(state_cols.reshape((-1,) + state_cols.shape[2:]), (1, 2, 3, 0))

    flat_units = slot_unit.reshape(-1)
    slot_total = slot_unit.shape[1]
    filled = (jnp.arange(slot_total, dtype=jnp.int32)[None, :] < unit_count[:, None]).reshape(-1)
    forward_table, inverse_table = slot_tables(flat_units, filled, step_count)

    outgoing = jnp.einsum(
        "tsp,tfyx->spfyx", forward_table, resid_cols, precision=lax.Precision.HIGH
    )
    pads = ((0, 0), (0, 0), (0, 0), (keep, keep), (0, 0))
    wide_source = jnp.pad(jnp.transpose(to_owners(outgoing), (0, 2, 1, 3, 4)), pads)

    own_units = lax.dynamic_index_in_dim(slot_unit, position, 0, keepdims=False)
    own_filled = lax.dynamic_index_in_dim(filled.reshape(groups, -1), position, 0, keepdims=False)
    coeffs = unit_inverse(own_units, step_count)

    global_row = lat_pos * rows - width + jnp.arange(rows + 2 * width, dtype=jnp.int32)
    row_mask = ((global_row >= 0) & (global_row < rows * lat_count)).astype(jnp.float32)
    solved = chebyshev(wide_source, wide_start, wide_depth, coeffs, row_mask[:, None])
    solved = solved[:, :, :, width : width + rows]
    spectrum = jnp.where(own_filled[:, None, None, None, None], solved, 0.0)

    turned = jnp.transpose(solved, (0, 2, 1, 3, 4))
    flat_solved = turned.reshape((1, -1, turned.shape[-1]))
    solved_cols = lax.all_to_all(flat_solved, "tm", split_axis=2, concat_axis=0, tiled=True)
    solved_cols = solved_cols.reshape(
        (groups * turned.shape[0],) + turned.shape[1:4] + (solved_cols.shape[-1],)
    )
    corr = jnp.einsum(
        "spfyx,tsp->fyxt", solved_cols, inverse_table, precision=lax.Precision.HIGH
    )
    updated = state_cols + corr
    return (updated, spectrum)


def solution(mesh):
    return jax.shard_map(
        body,
        mesh=mesh,
        in_specs=(
            P("tm", None, "lat", None),
            P("tm", None, "lat", None),
            P(None, "lat", None),
            P("lat", None),
            P("tm", None, None, "lat", None),
            P(),
            P(),
        ),
        out_specs=(P(None, "lat", "tm", None), P("tm", None, None, "lat", None)),
        check_vma=False,
    )
```

```python
import math

import jax
import jax.numpy as jnp
from jax import lax
from jax.sharding import PartitionSpec as P

SWEEPS = 6


HALF_COUPLING = 0.125
CORIOLIS = 0.2
FRICTION = 1.0
ALPHA = 0.1
SPREAD = 0.2


def with_halo(cells, sides, width):
    for axis, dim in sides:
        count = lax.axis_size(axis)
        ends = count - 1
        head = lax.slice_in_dim(cells, 0, width, axis=dim)
        tail = lax.slice_in_dim(cells, cells.shape[dim] - width, cells.shape[dim], axis=dim)
        cells = jnp.concatenate(
            [
                lax.ppermute(tail, axis, [(i, (i + 1) % count) for i in range(ends)]),
                cells,
                lax.ppermute(head, axis, [((i + 1) % count, i) for i in range(ends)]),
            ],
            axis=dim,
        )
    return cells


def shifted(value, axis, by):
    size = lax.axis_size(axis)
    pairs = [(i, i + by) for i in range(size) if 0 <= i + by < size]
    return lax.ppermute(value, axis, pairs)


def flux_operator(state, depth, pad_rule, row_mask=None):
    height = state[..., 0:1, :, :, :]
    east = state[..., 1:2, :, :, :]
    north = state[..., 2:3, :, :, :]
    if row_mask is not None:
        height = height * row_mask
    flux = jnp.concatenate([height, depth * east, depth * north], axis=-4)
    padded = pad_rule(flux)
    grad_x = padded[..., 0:1, :, 1:-1, 2:] - padded[..., 0:1, :, 1:-1, :-2]
    grad_y = padded[..., 0:1, :, 2:, 1:-1] - padded[..., 0:1, :, :-2, 1:-1]
    diverge = (
        padded[..., 1:2, :, 1:-1, 2:]
        - padded[..., 1:2, :, 1:-1, :-2]
        + (padded[..., 2:3, :, 2:, 1:-1] - padded[..., 2:3, :, :-2, 1:-1])
    )
    new_height = HALF_COUPLING * diverge
    new_east = HALF_COUPLING * grad_x - CORIOLIS * north
    new_north = HALF_COUPLING * grad_y + CORIOLIS * east
    return jnp.concatenate([new_height, new_east, new_north], axis=-4)


def row_rims(flux):
    rows_done = with_halo(flux, (("lat", 3),), 1)
    return jnp.pad(rows_done, ((0, 0), (0, 0), (0, 0), (0, 0), (1, 1)))


def zero_rim(values):
    widths = [(0, 0)] * (values.ndim - 2) + [(1, 1), (1, 1)]
    return jnp.pad(values, widths)


def to_owners(slots):
    return lax.all_to_all(slots, "tm", split_axis=0, concat_axis=4, tiled=True)


def from_owners(slots):
    return lax.all_to_all(slots, "tm", split_axis=4, concat_axis=0, tiled=True)


def slot_tables(units, filled, step_count):
    index_t = jnp.arange(step_count, dtype=jnp.int32)
    phases = index_t[:, None] * units[None, :] % step_count
    angles = phases.astype(jnp.float32) * (2.0 * math.pi / step_count)
    cosine = jnp.cos(angles)
    sine = jnp.sin(angles)
    parity = (1 - 2 * (index_t % 2)).astype(jnp.float32)
    first = units == 0
    times = index_t.astype(jnp.float32) / step_count
    damping = jnp.exp(times * math.log(ALPHA)) / math.sqrt(step_count)
    growth = jnp.exp(-times * math.log(ALPHA)) / math.sqrt(step_count)
    forward_imag = jnp.where(first[None, :], parity[:, None], -sine)
    forward_table = jnp.stack([cosine, forward_imag], axis=2) * damping[:, None, None]
    weights = jnp.where(first, 1.0, 2.0).astype(jnp.float32)
    inverse_real = cosine * weights[None, :]
    inverse_imag = jnp.where(first[None, :], parity[:, None], -2.0 * sine)
    keep = filled.astype(jnp.float32)[None, :, None]
    inverse_table = jnp.stack([inverse_real, inverse_imag], axis=2) * growth[:, None, None] * keep
    return (forward_table, inverse_table)


def unit_inverse(pair_ids, step_count):
    angles = pair_ids.astype(jnp.float32) * (2.0 * math.pi / step_count)
    ratio = math.exp(math.log(ALPHA) / step_count)
    real_shift = 1.0 + FRICTION - ratio * jnp.cos(angles)
    imag_shift = ratio * jnp.sin(angles)
    denominator = real_shift * real_shift + imag_shift * imag_shift
    real_inv = real_shift / denominator
    imag_inv = -imag_shift / denominator
    is_first = pair_ids == 0
    upper_left = jnp.where(is_first, 1.0 / (1.0 + FRICTION - ratio), real_inv)
    upper_right = jnp.where(is_first, 0.0, -imag_inv)
    lower_left = jnp.where(is_first, 0.0, imag_inv)
    lower_right = jnp.where(is_first, 1.0 / (1.0 + FRICTION + ratio), real_inv)
    return (upper_left, upper_right, lower_left, lower_right)


def apply_inverse(coeffs, values):
    shaped = [c[:, None, None, None] for c in coeffs]
    real_part = values[:, :, 0]
    imag_part = values[:, :, 1]
    new_real = shaped[0] * real_part + shaped[1] * imag_part
    new_imag = shaped[2] * real_part + shaped[3] * imag_part
    return jnp.stack([new_real, new_imag], axis=2)


def chebyshev(source, start, depth, coeffs, row_mask):
    iterate = start
    for sweep in range(SWEEPS):
        weight = 1.0 / (1.0 + SPREAD * math.cos(math.pi * (2 * sweep + 1) / (2 * SWEEPS)))
        flux = flux_operator(iterate, depth, zero_rim, row_mask)
        update = apply_inverse(coeffs, source - flux) - iterate
        iterate = iterate + weight * update
    return iterate


def lat_halo(arrays, width, sent):
    flat = [a.reshape((-1,) + a.shape[-2:]) for a in arrays]
    packed = jnp.concatenate(flat, axis=0)
    rows = packed.shape[1]
    count = lax.axis_size("lat")
    above = lax.ppermute(packed[:, rows - sent :], "lat", [(i, i + 1) for i in range(count - 1)])
    below = lax.ppermute(packed[:, :sent], "lat", [(i + 1, i) for i in range(count - 1)])
    blank = jnp.zeros((packed.shape[0], width - sent, packed.shape[2]), packed.dtype)
    wide = jnp.concatenate([blank, above, packed, below, blank], axis=1)
    out, offset = [], 0
    for a, f in zip(arrays, flat):
        piece = wide[offset : offset + f.shape[0]]
        out.append(piece.reshape(a.shape[:-2] + piece.shape[1:]))
        offset += f.shape[0]
    return out


def body(trajectory, forcing, initial_state, depth, warm_start, slot_unit, unit_count):
    groups = lax.axis_size("tm")
    position = lax.axis_index("tm")
    local_steps = trajectory.shape[0]
    step_count = local_steps * groups
    rows = depth.shape[0]
    lat_count = lax.axis_size("lat")
    lat_pos = lax.axis_index("lat")
    width = 8 * ((SWEEPS + 7) // 8)

    wide_traj, wide_forcing, wide_initial, wide_depth = lat_halo(
        [trajectory, forcing, initial_state, depth], width, SWEEPS
    )
    flux_term = flux_operator(wide_traj[:, :, None], wide_depth, zero_rim)[:, :, 0]
    partial = wide_forcing - ((1.0 + FRICTION) * wide_traj + flux_term)
    keep = width - SWEEPS + 1
    band = slice(keep, rows + 2 * width - keep)
    band_traj = wide_traj[:, :, band]
    band_part = partial[:, :, band]
    payload = jnp.concatenate(
        [
            wide_traj[0, :, width : width + rows],
            band_traj[1],
            band_part[0],
            band_part[1] + band_traj[0],
        ],
        axis=1,
    )
    outgoing_rows, warm_start = lax.optimization_barrier((payload[None], warm_start))
    (wide_start,) = lat_halo([warm_start], width, SWEEPS)
    moved = lax.all_to_all(outgoing_rows, "tm", split_axis=3, concat_axis=0, tiled=True)
    band_rows = band_traj.shape[2]
    first = moved[:, :, :rows]
    second = moved[:, :, rows : rows + band_rows]
    even_part = moved[:, :, rows + band_rows : rows + 2 * band_rows]
    odd_resid = moved[:, :, rows + 2 * band_rows :]
    col_count = moved.shape[3]
    initial_cols = lax.dynamic_slice_in_dim(
        wide_initial[:, band], position * col_count, col_count, axis=2
    )
    previous = jnp.concatenate([initial_cols[None], second[:-1]], axis=0)
    resid_cols = jnp.stack([even_part + previous, odd_resid], axis=1)
    resid_cols = resid_cols.reshape((-1,) + resid_cols.shape[2:])
    inner = width - keep
    state_cols = jnp.stack([first, second[:, :, inner : inner + rows]], axis=1)
    state_cols = jnp.transpose(state_cols.reshape((-1,) + state_cols.shape[2:]), (1, 2, 3, 0))

    flat_units = slot_unit.reshape(-1)
    slot_total = slot_unit.shape[1]
    filled = (jnp.arange(slot_total, dtype=jnp.int32)[None, :] < unit_count[:, None]).reshape(-1)
    forward_table, inverse_table = slot_tables(flat_units, filled, step_count)

    outgoing = jnp.einsum(
        "tsp,tfyx->fpyxs", forward_table, resid_cols, precision=lax.Precision.HIGH
    )
    pads = ((0, 0), (0, 0), (0, 0), (keep, keep), (0, 0))
    received = lax.all_to_all(
        outgoing.reshape((1, -1, outgoing.shape[-1])), "tm", split_axis=2, concat_axis=0, tiled=True
    )
    received = received.reshape((groups,) + outgoing.shape[:4] + (-1,))
    owned = jnp.transpose(received, (5, 1, 2, 3, 0, 4))
    wide_source = jnp.pad(owned.reshape(owned.shape[:4] + (-1,)), pads)

    own_units = lax.dynamic_index_in_dim(slot_unit, position, 0, keepdims=False)
    own_filled = lax.dynamic_index_in_dim(filled.reshape(groups, -1), position, 0, keepdims=False)
    coeffs = unit_inverse(own_units, step_count)

    global_row = lat_pos * rows - width + jnp.arange(rows + 2 * width, dtype=jnp.int32)
    row_mask = ((global_row >= 0) & (global_row < rows * lat_count)).astype(jnp.float32)
    solved = chebyshev(wide_source, wide_start, wide_depth, coeffs, row_mask[:, None])
    solved = solved[:, :, :, width : width + rows]
    spectrum = jnp.where(own_filled[:, None, None, None, None], solved, 0.0)

    turned = jnp.transpose(solved, (0, 2, 1, 3, 4))
    flat_solved = turned.reshape((1, -1, turned.shape[-1]))
    solved_cols = lax.all_to_all(flat_solved, "tm", split_axis=2, concat_axis=0, tiled=True)
    solved_cols = solved_cols.reshape(
        (groups * turned.shape[0],) + turned.shape[1:4] + (solved_cols.shape[-1],)
    )
    corr = jnp.einsum(
        "spfyx,tsp->fyxt", solved_cols, inverse_table, precision=lax.Precision.HIGH
    )
    updated = state_cols + corr
    return (updated, spectrum)


def solution(mesh):
    return jax.shard_map(
        body,
        mesh=mesh,
        in_specs=(
            P("tm", None, "lat", None),
            P("tm", None, "lat", None),
            P(None, "lat", None),
            P("lat", None),
            P("tm", None, None, "lat", None),
            P(),
            P(),
        ),
        out_specs=(P(None, "lat", "tm", None), P("tm", None, None, "lat", None)),
        check_vma=False,
    )
```
